256 devices in a mesh: dom: 128 (over y, x, z), sub: 2 (over core).
Axes of the slice: x: 4, y: 4, z: 8, core: 2. Of those that a mesh axis runs over, the one named last changes fastest.
Arguments:
- codes: int32 [65536, 4], P(('dom', 'sub')), may hold values from 0 to 255
- books: bfloat16 [4, 256, 128], P('sub'), may hold values from -6 to 6
- alpha: float32 [512, 64], replicated, may hold values from -0.75 to 0.75
- basis: float32 [64, 512], replicated, may hold values from -6 to 6
- w_msg: bfloat16 [512, 512], replicated, may hold values from -0.25 to 0.25
- w_self: bfloat16 [512, 512], replicated, may hold values from -0.25 to 0.25
- tiles: bfloat16 [4096, 128, 128], P(('dom', 'sub')), may hold values from -0.1875 to 0.1875
- tile_src: int32 [4096], P(('dom', 'sub')), may hold values from 0 to 13
- tile_rel: int32 [4096], P(('dom', 'sub')), may hold values from 0 to 511
- send_rows: int32 [128, 2, 128, 8], P('dom', 'sub'), may hold values from 0 to 255
- send_count: int32 [128, 2, 128], P('dom', 'sub'), may hold values from 0 to 8, as said below
- hub_owner: int32 [2], replicated, may hold values from 0 to 127
- cotangent: bfloat16 [65536, 512], P(('dom', 'sub')), may hold values from -0.01171875 to 0.01171875
Outputs:
- output: bfloat16 [65536, 512], P(('dom', 'sub'))
- grad_w_msg: float32 [512, 512], replicated
- grad_w_self: float32 [512, 512], replicated
- grad_alpha: float32 [512, 64], replicated
- grad_basis: float32 [64, 512], replicated
- grad_books: float32 [4, 256, 128], P('sub')
The draws below stay inside these ranges and needn't reach their ends.
Inputs may be any that keep to these rules, and one draw needn't show every extreme that they name: `send_count`: every device uses all 8 slots toward at least one partition.
All inputs are finite; a program needn't handle non-finite values.
Results may differ from the reference program's by a relative error of at most 0.015.
Values may be sent and summed in bfloat16 or wider, within the bound.
No kernel may reach another device: no remote copies, remote signals or barrier semaphores. Data moves between devices by JAX's collectives and lax.ppermute only.
A program may use at most 64 MiB of HBM per device.

```python
import jax
import jax.numpy as jnp
from jax import lax

D = 512
NBASIS = 64
NREL = 512
NBOOK = 4
KCODE = 256
ROWS_DEV = 256
TB = 128
TPB = 8
SLOT = 8
HUB = 256
NHUB = 2
NPART = 128
NSUBS = 2
DEVS = 256
ENT = 65536
NBLK = 2
NTILE = 16
TILES = 4096
NSRC = 14


def draw_send_count(key, part):
    counts = jax.random.randint(key, (NPART, NSUBS, NPART), 0, SLOT + 1)
    filled = jax.random.randint(jax.random.fold_in(key, 7), (NPART, NSUBS, 1), 0, NPART)
    spots = jnp.arange(NPART, dtype=jnp.int32)[None, None, :]
    return jnp.where(spots == filled, SLOT, counts).astype(jnp.int32)


def with_ends(values, key, least, high):
    longest = values.shape.index(max(values.shape))
    spots = []
    for shift in (0, 1):
        where = [jax.random.randint(jax.random.fold_in(key, axis), (), 0, length) for axis, length in enumerate(values.shape)]
        where[longest] = (where[longest] + shift) % values.shape[longest]
        spots.append(tuple(where))
    return values.at[spots[0]].set(least).at[spots[1]].set(high)


def block_levels(stream_key, shape, cuts, smallest, high):
    factor_of, own = 1.0, jax.random.fold_in(stream_key, 6)
    for dim, parts in cuts:
        draws = jnp.exp(jax.random.uniform(jax.random.fold_in(own, dim), (parts,), jnp.float32, smallest / len(cuts), high / len(cuts)))
        factor_of = factor_of * jnp.repeat(draws, shape[dim] // parts).reshape([-1 if axis == dim else 1 for axis in range(len(shape))])
    return factor_of


def scatter_about(key, extent, spread, bound, shards=(), kind=jnp.bfloat16):
    entries = jax.random.normal(key, extent, jnp.float32) * spread
    if len(shards) > 0:
        entries = block_levels(key, extent, shards, -0.22, 0.18) * entries
    return jnp.clip(entries, min=-bound, max=bound).astype(kind)


def setup_inputs(seed: int = 0) -> dict:
    key_list = jax.random.split(jax.random.key(seed), 14)
    return {
        "codes": with_ends(jax.random.randint(key_list[0], (ENT, NBOOK), 0, KCODE), jax.random.fold_in(key_list[0], 1), 0, KCODE - 1).astype(jnp.int32),
        "books": scatter_about(key_list[1], (NBOOK, KCODE, D // NBOOK), 1.0, 6.0, ((0, 2),)),
        "alpha": scatter_about(key_list[2], (NREL, NBASIS), NBASIS ** -0.5, 0.75, (), jnp.float32),
        "basis": scatter_about(key_list[3], (NBASIS, D), 1.0, 6.0, (), jnp.float32),
        "w_msg": scatter_about(key_list[4], (D, D), D ** -0.5, 0.25),
        "w_self": scatter_about(key_list[5], (D, D), D ** -0.5, 0.25),
        "tiles": scatter_about(key_list[6], (TILES, TB, TB), (TB * TPB) ** -0.5, 0.1875, ((0, 256),)),
        "tile_src": with_ends(jax.random.randint(key_list[7], (TILES,), 0, NSRC), jax.random.fold_in(key_list[7], 1), 0, NSRC - 1).astype(jnp.int32),
        "tile_rel": with_ends(jax.random.randint(key_list[8], (TILES,), 0, NREL), jax.random.fold_in(key_list[8], 1), 0, NREL - 1).astype(jnp.int32),
        "send_rows": with_ends(jax.random.randint(key_list[9], (NPART, NSUBS, NPART, SLOT), 0, ROWS_DEV), jax.random.fold_in(key_list[9], 1), 0, ROWS_DEV - 1).astype(jnp.int32),
        "send_count": draw_send_count(jax.random.fold_in(key_list[13], 71), 0),
        "hub_owner": jax.random.randint(key_list[11], (NHUB,), 0, NPART).astype(jnp.int32),
        "cotangent": scatter_about(key_list[12], (ENT, D), 0.002, 0.01171875, ((0, 256),)),
    }


HIGHEST_PREC = lax.Precision.HIGHEST


def decode_rows(code_rows, books):
    picked = books[jnp.arange(NBOOK)[None, :], code_rows]
    return picked.reshape(code_rows.shape[0], D)


def reference(codes, books, alpha, basis, w_msg, w_self, tiles, tile_src, tile_rel, send_rows, send_count, hub_owner, cotangent):
    slice_width = D // NBOOK
    features = decode_rows(codes, books)
    feat_dev = features.reshape(NPART, NSUBS, ROWS_DEV, D)
    code_dev = codes.reshape(NPART, NSUBS, ROWS_DEV, NBOOK)
    rel_table = jnp.dot(alpha, basis, precision=HIGHEST_PREC, preferred_element_type=jnp.float32)
    tiles_dev = tiles.reshape(DEVS, NTILE, TB, TB)
    source_dev = tile_src.reshape(DEVS, NTILE)
    relation_dev = tile_rel.reshape(DEVS, NTILE)
    peer_ids = jnp.arange(NPART, dtype=jnp.int32)

    def sources(device):
        dom_index = device // NSUBS
        sub_index = device % NSUBS
        row_index = send_rows[:, sub_index, dom_index, :]
        slot_valid = jnp.arange(SLOT, dtype=jnp.int32)[None, :] < send_count[:, sub_index, dom_index][:, None]
        received = jnp.where(slot_valid[:, :, None], feat_dev[peer_ids[:, None], sub_index, row_index], jnp.zeros((), jnp.bfloat16))
        recv_codes = jnp.where(slot_valid[:, :, None], code_dev[peer_ids[:, None], sub_index, row_index], -1)
        hub_rows = feat_dev[hub_owner, sub_index, :HUB]
        hub_codes = code_dev[hub_owner, sub_index, :HUB]
        table = jnp.concatenate([feat_dev[dom_index, sub_index], received.reshape(-1, D), hub_rows.reshape(-1, D)], axis=0)
        lookup_table_codes = jnp.concatenate([code_dev[dom_index, sub_index], recv_codes.reshape(-1, NBOOK), hub_codes.reshape(-1, NBOOK)], axis=0)
        return table, lookup_table_codes

    def forward(device):
        table, lookup_table_codes = sources(device)
        blocks = table.reshape(NSRC, TB, D)
        picked = blocks[source_dev[device]].astype(jnp.float32)
        composed = (picked * rel_table[relation_dev[device]][:, None, :]).astype(jnp.bfloat16)
        partial_terms = jnp.einsum('tij,tjd->tid', tiles_dev[device].astype(jnp.float32), composed.astype(jnp.float32))
        return partial_terms.reshape(NBLK, TPB, TB, D).sum(axis=1).reshape(ROWS_DEV, D).astype(jnp.bfloat16)

    aggregate = lax.map(forward, jnp.arange(DEVS, dtype=jnp.int32)).reshape(ENT, D)
    pre_act = jnp.dot(aggregate, w_msg, preferred_element_type=jnp.float32) + jnp.dot(features, w_self, preferred_element_type=jnp.float32)
    activated = jnp.tanh(pre_act)
    output = activated.astype(jnp.bfloat16)
    grad_pre = (cotangent.astype(jnp.float32) * (1.0 - activated * activated)).astype(jnp.bfloat16)
    grad_w_msg = jnp.dot(aggregate.T, grad_pre, preferred_element_type=jnp.float32)
    grad_w_self = jnp.dot(features.T, grad_pre, preferred_element_type=jnp.float32)
    grad_agg = jnp.dot(grad_pre, w_msg.T, preferred_element_type=jnp.float32).astype(jnp.bfloat16)
    grad_self = jnp.dot(grad_pre, w_self.T, preferred_element_type=jnp.float32)
    grad_agg_dev = grad_agg.reshape(DEVS, NBLK, TB, D)
    grad_self_dev = grad_self.reshape(DEVS, ROWS_DEV, D)

    def backward(carry, device):
        rel_grad, book_grad = carry
        table, lookup_table_codes = sources(device)
        blocks = table.reshape(NSRC, TB, D)
        source_ids = source_dev[device]
        relation_ids = relation_dev[device]
        picked = blocks[source_ids].astype(jnp.float32)
        upstream = jnp.repeat(grad_agg_dev[device], TPB, axis=0).astype(jnp.float32)
        grad_comp = jnp.einsum('tji,tjd->tid', tiles_dev[device].astype(jnp.float32), upstream)
        rel_grad = rel_grad.at[relation_ids].add(jnp.sum(grad_comp * picked, axis=1))
        grad_blocks = jnp.zeros((NSRC, TB, D), jnp.float32).at[source_ids].add(grad_comp * rel_table[relation_ids][:, None, :])
        grad_rows = grad_blocks.reshape(NSRC * TB, D)
        grad_rows = grad_rows.at[:ROWS_DEV].add(grad_self_dev[device])
        for book_index in range(NBOOK):
            piece = grad_rows[:, book_index * slice_width:(book_index + 1) * slice_width]
            book_grad = book_grad.at[book_index].add(jax.ops.segment_sum(piece, lookup_table_codes[:, book_index], num_segments=KCODE))
        return (rel_grad, book_grad), None

    start_carry = (jnp.zeros((NREL, D), jnp.float32), jnp.zeros((NBOOK, KCODE, slice_width), jnp.float32))
    final_carry = lax.scan(backward, start_carry, jnp.arange(DEVS, dtype=jnp.int32))[0]
    rel_grad, grad_books = final_carry
    grad_alpha = jnp.dot(rel_grad, basis.T, precision=HIGHEST_PREC, preferred_element_type=jnp.float32)
    grad_basis = jnp.dot(alpha.T, rel_grad, precision=HIGHEST_PREC, preferred_element_type=jnp.float32)
    return (output, grad_w_msg, grad_w_self, grad_alpha, grad_basis, grad_books)
```

```python
import jax
import jax.numpy as jnp
from jax import lax
from jax.sharding import PartitionSpec as P

TB = 128
TPB = 8
SLOT = 8
NHUB = 2


HIGHEST_PREC = lax.Precision.HIGHEST


def one_hot_codes(code_rows, code_count, out_type):
    return (code_rows[..., None] == jnp.arange(code_count, dtype=jnp.int32)).astype(out_type)


def decode(code_rows, complete_codebooks):
    indicator_rows = one_hot_codes(code_rows, complete_codebooks.shape[1], jnp.bfloat16)
    rows = jnp.einsum(
        "feu,euq->feq", indicator_rows, complete_codebooks, preferred_element_type=jnp.float32
    )
    return rows.astype(jnp.bfloat16).reshape(code_rows.shape[0], -1)


def fold_books(code_rows, gradients, code_count):
    book_count = code_rows.shape[1]
    indicator_rows = one_hot_codes(code_rows, code_count, jnp.bfloat16)
    pieces = gradients.reshape(gradients.shape[0], book_count, -1)
    upper_bound = pieces.astype(jnp.bfloat16)
    lower_bound = (pieces - upper_bound.astype(jnp.float32)).astype(jnp.bfloat16)
    upper_half_sum = jnp.einsum(
        "fco,fcg->cog", indicator_rows, upper_bound, preferred_element_type=jnp.float32
    )
    lower_half_sum = jnp.einsum(
        "fco,fcg->cog", indicator_rows, lower_bound, preferred_element_type=jnp.float32
    )
    return upper_half_sum + lower_half_sum


def all_sum(parts, axes, n_dev):
    flat = jnp.concatenate([p.reshape(-1) for p in parts])
    size = flat.shape[0]
    padded = -(-size // n_dev) * n_dev
    flat = jnp.pad(flat, (0, padded - size))
    chunks = flat.reshape(n_dev, -1)
    received = lax.all_to_all(chunks, axes, 0, 0, tiled=True)
    mine = jnp.sum(received, axis=0)
    spread = jnp.broadcast_to(mine[None], chunks.shape)
    total = lax.all_to_all(spread, axes, 0, 0, tiled=True).reshape(-1)[:size]
    out = []
    start = 0
    for p in parts:
        out.append(total[start : start + p.size].reshape(p.shape))
        start += p.size
    return out


def shards(
    n_dev,
    codes,
    books,
    alpha,
    basis,
    w_msg,
    w_self,
    tiles,
    tile_src,
    tile_rel,
    send_rows,
    send_count,
    hub_owner,
    cotangent,
):
    rows_dev, book_count = codes.shape
    code_count = books.shape[1]
    model_width = w_msg.shape[0]
    tile_count = tiles.shape[0]
    block_count = tile_count // TPB
    complete_codebooks = lax.all_gather(books, "sub", axis=0, tiled=True)
    rel_table = jnp.dot(alpha, basis, precision=HIGHEST_PREC, preferred_element_type=jnp.float32)
    targets = send_rows[0, 0]
    part_count = targets.shape[0]
    frag = rows_dev // part_count
    slot_valid = jnp.arange(SLOT, dtype=jnp.int32)[None, :] < send_count[0, 0][:, None]
    out_codes = jnp.where(slot_valid[:, :, None], codes[targets], -1)
    hub_piece = codes.reshape(part_count, frag, book_count)
    payload = jnp.concatenate([out_codes, hub_piece], axis=1)
    incoming = lax.all_to_all(payload, "dom", 0, 0, tiled=True)
    recv_codes = incoming[:, :SLOT].reshape(-1, book_count)
    held = jnp.concatenate(
        [incoming[hub_owner[hub_index], SLOT:] for hub_index in range(NHUB)], axis=0
    )
    spread = jnp.broadcast_to(held[None], (part_count,) + held.shape)
    gathered = lax.all_to_all(spread, "dom", 0, 0, tiled=True)
    hub_codes = [
        gathered[:, hub_index * frag : (hub_index + 1) * frag].reshape(-1, book_count)
        for hub_index in range(NHUB)
    ]
    table_codes = jnp.concatenate([codes, recv_codes] + hub_codes, axis=0)
    table = decode(table_codes, complete_codebooks)
    local_rows = table[:rows_dev]
    blocks = table.reshape(-1, TB, model_width)
    tile_blocks = tiles.reshape(block_count, TPB, TB, TB)
    source_blocks = tile_src.reshape(block_count, TPB)
    relation_blocks = tile_rel.reshape(block_count, TPB)

    def forward_block(packed):
        weights_now, source_now, relation_now = packed
        composed = (
            blocks[source_now].astype(jnp.float32) * rel_table[relation_now][:, None, :]
        ).astype(jnp.bfloat16)
        summed = jnp.einsum(
            "tij,tjd->id", weights_now, composed, preferred_element_type=jnp.float32
        )
        return summed.astype(jnp.bfloat16)

    aggregate = lax.map(forward_block, (tile_blocks, source_blocks, relation_blocks)).reshape(
        rows_dev, model_width
    )
    pre_act = jnp.dot(aggregate, w_msg, preferred_element_type=jnp.float32) + jnp.dot(
        local_rows, w_self, preferred_element_type=jnp.float32
    )
    activated = jnp.tanh(pre_act)
    output = activated.astype(jnp.bfloat16)
    grad_pre = (cotangent.astype(jnp.float32) * (1.0 - activated * activated)).astype(jnp.bfloat16)
    contract_rows = (((0,), (0,)), ((), ()))
    contract_cols = (((1,), (1,)), ((), ()))
    grad_w_msg = lax.dot_general(
        aggregate, grad_pre, contract_rows, preferred_element_type=jnp.float32
    )
    grad_w_self = lax.dot_general(
        local_rows, grad_pre, contract_rows, preferred_element_type=jnp.float32
    )
    grad_agg = lax.dot_general(
        grad_pre, w_msg, contract_cols, preferred_element_type=jnp.float32
    ).astype(jnp.bfloat16)
    grad_self = lax.dot_general(grad_pre, w_self, contract_cols, preferred_element_type=jnp.float32)
    grad_blocks = grad_agg.reshape(block_count, TB, model_width)

    def backward_block(carry, packed):
        table_grad, rel_grad = carry
        weights_now, source_now, relation_now, upstream = packed
        grad_comp = jnp.einsum(
            "tji,jd->tid", weights_now, upstream, preferred_element_type=jnp.float32
        )
        rel_grad = rel_grad.at[relation_now].add(
            jnp.sum(grad_comp * blocks[source_now].astype(jnp.float32), axis=1)
        )
        table_grad = table_grad.at[source_now].add(grad_comp * rel_table[relation_now][:, None, :])
        return ((table_grad, rel_grad), None)

    start_carry = (jnp.zeros(blocks.shape, jnp.float32), jnp.zeros(rel_table.shape, jnp.float32))
    final_carry = lax.scan(
        backward_block, start_carry, (tile_blocks, source_blocks, relation_blocks, grad_blocks)
    )[0]
    table_grad, rel_grad = final_carry
    table_grad = table_grad.reshape(-1, model_width)
    table_grad = table_grad.at[:rows_dev].add(grad_self)
    book_grad = fold_books(table_codes, table_grad, code_count)
    part_alpha = jnp.dot(
        rel_grad, basis.T, precision=HIGHEST_PREC, preferred_element_type=jnp.float32
    )
    part_basis = jnp.dot(
        alpha.T, rel_grad, precision=HIGHEST_PREC, preferred_element_type=jnp.float32
    )
    total_msg, total_self, grad_alpha, grad_basis, total_books = all_sum(
        (grad_w_msg, grad_w_self, part_alpha, part_basis, book_grad), ("dom", "sub"), n_dev
    )
    book_share = books.shape[0]
    grad_books = lax.dynamic_slice_in_dim(
        total_books, lax.axis_index("sub") * book_share, book_share, 0
    )
    return (output, total_msg, total_self, grad_alpha, grad_basis, grad_books)


def solution(mesh):
    n_dev = mesh.shape["dom"] * mesh.shape["sub"]

    def run(*args):
        return shards(n_dev, *args)

    return jax.shard_map(
        run,
        mesh=mesh,
        in_specs=(
            P(("dom", "sub"), None),
            P("sub", None, None),
            P(),
            P(),
            P(),
            P(),
            P(("dom", "sub"), None, None),
            P(("dom", "sub")),
            P(("dom", "sub")),
            P("dom", "sub", None, None),
            P("dom", "sub", None),
            P(),
            P(("dom", "sub"), None),
        ),
        out_specs=(P(("dom", "sub"), None), P(), P(), P(), P(), P("sub", None, None)),
        check_vma=False,
    )
```

```python
import jax
import jax.numpy as jnp
from jax import lax
from jax.sharding import PartitionSpec as P

TB = 128
TPB = 8
SLOT = 8
NHUB = 2


HIGHEST_PREC = lax.Precision.HIGHEST


def one_hot_codes(code_rows, code_count, out_type):
    return (code_rows[..., None] == jnp.arange(code_count, dtype=jnp.int32)).astype(out_type)


def decode(code_rows, complete_codebooks):
    indicator_rows = one_hot_codes(code_rows, complete_codebooks.shape[1], jnp.bfloat16)
    rows = jnp.einsum(
        "feu,euq->feq", indicator_rows, complete_codebooks, preferred_element_type=jnp.float32
    )
    return rows.astype(jnp.bfloat16).reshape(code_rows.shape[0], -1)


def fold_books(code_rows, gradients, code_count):
    book_count = code_rows.shape[1]
    indicator_rows = one_hot_codes(code_rows, code_count, jnp.bfloat16)
    pieces = gradients.reshape(gradients.shape[0], book_count, -1)
    upper_bound = pieces.astype(jnp.bfloat16)
    lower_bound = (pieces - upper_bound.astype(jnp.float32)).astype(jnp.bfloat16)
    upper_half_sum = jnp.einsum(
        "fco,fcg->cog", indicator_rows, upper_bound, preferred_element_type=jnp.float32
    )
    lower_half_sum = jnp.einsum(
        "fco,fcg->cog", indicator_rows, lower_bound, preferred_element_type=jnp.float32
    )
    return upper_half_sum + lower_half_sum


def all_sum(parts, n_dom):
    flat = jnp.concatenate([p.reshape(-1) for p in parts])
    size = flat.shape[0]
    unit = 2 * n_dom
    padded = -(-size // unit) * unit
    halves = jnp.pad(flat, (0, padded - size)).reshape(2, -1)
    sub_index = lax.axis_index("sub")
    keep = lax.dynamic_index_in_dim(halves, sub_index, 0, keepdims=False)
    give = lax.dynamic_index_in_dim(halves, 1 - sub_index, 0, keepdims=False)
    swap = [(0, 1), (1, 0)]
    mine = keep + lax.ppermute(give, "sub", swap)
    chunks = mine.reshape(n_dom, -1)
    received = lax.all_to_all(chunks, "dom", 0, 0, tiled=True)
    reduced = jnp.sum(received, axis=0).astype(jnp.bfloat16)
    spread = jnp.broadcast_to(reduced[None], chunks.shape)
    own_half = lax.all_to_all(spread, "dom", 0, 0, tiled=True).reshape(-1)
    other_half = lax.ppermute(own_half, "sub", swap)
    both = jnp.zeros(halves.shape, jnp.bfloat16)
    both = lax.dynamic_update_index_in_dim(both, own_half, sub_index, 0)
    both = lax.dynamic_update_index_in_dim(both, other_half, 1 - sub_index, 0)
    total = both.reshape(-1)[:size].astype(jnp.float32)
    out = []
    start = 0
    for p in parts:
        out.append(total[start : start + p.size].reshape(p.shape))
        start += p.size
    return out


def shards(
    n_dom,
    codes,
    books,
    alpha,
    basis,
    w_msg,
    w_self,
    tiles,
    tile_src,
    tile_rel,
    send_rows,
    send_count,
    hub_owner,
    cotangent,
):
    rows_dev, book_count = codes.shape
    code_count = books.shape[1]
    model_width = w_msg.shape[0]
    tile_count = tiles.shape[0]
    block_count = tile_count // TPB
    complete_codebooks = lax.all_gather(books, "sub", axis=0, tiled=True)
    rel_table = jnp.dot(alpha, basis, precision=HIGHEST_PREC, preferred_element_type=jnp.float32)
    targets = send_rows[0, 0]
    part_count = targets.shape[0]
    slot_valid = jnp.arange(SLOT, dtype=jnp.int32)[None, :] < send_count[0, 0][:, None]
    out_codes = jnp.where(slot_valid[:, :, None], codes[targets], -1)
    own_codes = jnp.broadcast_to(codes[None], (part_count,) + codes.shape)
    payload = jnp.concatenate([out_codes, own_codes], axis=1)
    incoming = lax.all_to_all(payload, "dom", 0, 0, tiled=True)
    recv_codes = incoming[:, :SLOT].reshape(-1, book_count)
    hub_codes = [incoming[hub_owner[hub_index], SLOT:] for hub_index in range(NHUB)]
    table_codes = jnp.concatenate([codes, recv_codes] + hub_codes, axis=0)
    table = decode(table_codes, complete_codebooks)
    local_rows = table[:rows_dev]
    blocks = table.reshape(-1, TB, model_width)
    tile_blocks = tiles.reshape(block_count, TPB, TB, TB)
    source_blocks = tile_src.reshape(block_count, TPB)
    relation_blocks = tile_rel.reshape(block_count, TPB)

    def forward_block(packed):
        weights_now, source_now, relation_now = packed
        composed = (
            blocks[source_now].astype(jnp.float32) * rel_table[relation_now][:, None, :]
        ).astype(jnp.bfloat16)
        summed = jnp.einsum(
            "tij,tjd->id", weights_now, composed, preferred_element_type=jnp.float32
        )
        return summed.astype(jnp.bfloat16)

    aggregate = lax.map(forward_block, (tile_blocks, source_blocks, relation_blocks)).reshape(
        rows_dev, model_width
    )
    pre_act = jnp.dot(aggregate, w_msg, preferred_element_type=jnp.float32) + jnp.dot(
        local_rows, w_self, preferred_element_type=jnp.float32
    )
    activated = jnp.tanh(pre_act)
    output = activated.astype(jnp.bfloat16)
    grad_pre = (cotangent.astype(jnp.float32) * (1.0 - activated * activated)).astype(jnp.bfloat16)
    contract_rows = (((0,), (0,)), ((), ()))
    contract_cols = (((1,), (1,)), ((), ()))
    grad_w_msg = lax.dot_general(
        aggregate, grad_pre, contract_rows, preferred_element_type=jnp.float32
    )
    grad_w_self = lax.dot_general(
        local_rows, grad_pre, contract_rows, preferred_element_type=jnp.float32
    )
    grad_agg = lax.dot_general(
        grad_pre, w_msg, contract_cols, preferred_element_type=jnp.float32
    ).astype(jnp.bfloat16)
    grad_self = lax.dot_general(grad_pre, w_self, contract_cols, preferred_element_type=jnp.float32)
    grad_blocks = grad_agg.reshape(block_count, TB, model_width)

    def backward_block(carry, packed):
        table_grad, rel_grad = carry
        weights_now, source_now, relation_now, upstream = packed
        grad_comp = jnp.einsum(
            "tji,jd->tid", weights_now, upstream, preferred_element_type=jnp.float32
        )
        rel_grad = rel_grad.at[relation_now].add(
            jnp.sum(grad_comp * blocks[source_now].astype(jnp.float32), axis=1)
        )
        table_grad = table_grad.at[source_now].add(grad_comp * rel_table[relation_now][:, None, :])
        return ((table_grad, rel_grad), None)

    start_carry = (jnp.zeros(blocks.shape, jnp.float32), jnp.zeros(rel_table.shape, jnp.float32))
    final_carry = lax.scan(
        backward_block, start_carry, (tile_blocks, source_blocks, relation_blocks, grad_blocks)
    )[0]
    table_grad, rel_grad = final_carry
    table_grad = table_grad.reshape(-1, model_width)
    table_grad = table_grad.at[:rows_dev].add(grad_self)
    book_grad = fold_books(table_codes, table_grad, code_count)
    part_alpha = jnp.dot(
        rel_grad, basis.T, precision=HIGHEST_PREC, preferred_element_type=jnp.float32
    )
    part_basis = jnp.dot(
        alpha.T, rel_grad, precision=HIGHEST_PREC, preferred_element_type=jnp.float32
    )
    total_msg, total_self, grad_alpha, grad_basis, total_books = all_sum(
        (grad_w_msg, grad_w_self, part_alpha, part_basis, book_grad), n_dom
    )
    book_share = books.shape[0]
    grad_books = lax.dynamic_slice_in_dim(
        total_books, lax.axis_index("sub") * book_share, book_share, 0
    )
    return (output, total_msg, total_self, grad_alpha, grad_basis, grad_books)


def solution(mesh):
    n_dom = mesh.shape["dom"]

    def run(*args):
        return shards(n_dom, *args)

    return jax.shard_map(
        run,
        mesh=mesh,
        in_specs=(
            P(("dom", "sub"), None),
            P("sub", None, None),
            P(),
            P(),
            P(),
            P(),
            P(("dom", "sub"), None, None),
            P(("dom", "sub")),
            P(("dom", "sub")),
            P("dom", "sub", None, None),
            P("dom", "sub", None),
            P(),
            P(("dom", "sub"), None),
        ),
        out_specs=(P(("dom", "sub"), None), P(), P(), P(), P(), P("sub", None, None)),
        check_vma=False,
    )
```

```python
import jax
import jax.numpy as jnp
from jax import lax
from jax.sharding import PartitionSpec as P

TB = 128
TPB = 8
SLOT = 8
NHUB = 2


HIGHEST_PREC = lax.Precision.HIGHEST


def one_hot_codes(code_rows, code_count, out_type):
    return (code_rows[..., None] == jnp.arange(code_count, dtype=jnp.int32)).astype(out_type)


def decode(code_rows, complete_codebooks):
    indicator_rows = one_hot_codes(code_rows, complete_codebooks.shape[1], jnp.bfloat16)
    rows = jnp.einsum(
        "feu,euq->feq", indicator_rows, complete_codebooks, preferred_element_type=jnp.float32
    )
    return rows.astype(jnp.bfloat16).reshape(code_rows.shape[0], -1)


def fold_books(code_rows, gradients, code_count):
    book_count = code_rows.shape[1]
    indicator_rows = one_hot_codes(code_rows, code_count, jnp.bfloat16)
    pieces = gradients.reshape(gradients.shape[0], book_count, -1)
    upper_bound = pieces.astype(jnp.bfloat16)
    lower_bound = (pieces - upper_bound.astype(jnp.float32)).astype(jnp.bfloat16)
    upper_half_sum = jnp.einsum(
        "fco,fcg->cog", indicator_rows, upper_bound, preferred_element_type=jnp.float32
    )
    lower_half_sum = jnp.einsum(
        "fco,fcg->cog", indicator_rows, lower_bound, preferred_element_type=jnp.float32
    )
    return upper_half_sum + lower_half_sum


def all_sum(grad_w_msg, grad_w_self, part_alpha, part_basis, book_grad, n_dom):
    sub_index = lax.axis_index("sub")
    width = grad_w_msg.shape[1]
    share = book_grad.shape[0] // 2
    dense = [grad_w_msg, grad_w_self, part_basis, part_alpha.reshape(-1, width)]

    def half_of(h):
        pieces = [lax.dynamic_slice_in_dim(x, h * (x.shape[0] // 2), x.shape[0] // 2, 0) for x in dense]
        pieces.append(lax.dynamic_slice_in_dim(book_grad, h * share, share, 0).reshape(-1, width))
        return jnp.concatenate(pieces, axis=0)

    swap = [(0, 1), (1, 0)]
    mine = half_of(sub_index) + lax.ppermute(half_of(1 - sub_index), "sub", swap)
    rows = mine.shape[0]
    chunks = mine.reshape(n_dom, -1, 128)
    received = lax.all_to_all(chunks, "dom", 0, 0, tiled=True)
    reduced = jnp.sum(received, axis=0).astype(jnp.bfloat16)
    spread = jnp.broadcast_to(reduced[None], chunks.shape)
    own_half = lax.all_to_all(spread, "dom", 0, 0, tiled=True).reshape(rows, width)
    dense_rows = rows - share * book_grad.shape[1] * book_grad.shape[2] // width
    own_dense = own_half[:dense_rows]
    other_dense = lax.ppermute(own_dense, "sub", swap)
    low = jnp.where(sub_index == 0, own_dense, other_dense).astype(jnp.float32)
    high = jnp.where(sub_index == 0, other_dense, own_dense).astype(jnp.float32)
    out = []
    start = 0
    for x in dense:
        r = x.shape[0] // 2
        out.append(jnp.concatenate([low[start : start + r], high[start : start + r]], axis=0))
        start += r
    out[3] = out[3].reshape(part_alpha.shape)
    books_mine = own_half[dense_rows:].astype(jnp.float32).reshape((share,) + book_grad.shape[1:])
    return out + [books_mine]


def shards(
    n_dom,
    codes,
    books,
    alpha,
    basis,
    w_msg,
    w_self,
    tiles,
    tile_src,
    tile_rel,
    send_rows,
    send_count,
    hub_owner,
    cotangent,
):
    rows_dev, book_count = codes.shape
    code_count = books.shape[1]
    model_width = w_msg.shape[0]
    tile_count = tiles.shape[0]
    block_count = tile_count // TPB
    complete_codebooks = lax.all_gather(books, "sub", axis=0, tiled=True)
    rel_table = jnp.dot(alpha, basis, precision=HIGHEST_PREC, preferred_element_type=jnp.float32)
    targets = send_rows[0, 0]
    part_count = targets.shape[0]
    slot_valid = jnp.arange(SLOT, dtype=jnp.int32)[None, :] < send_count[0, 0][:, None]
    out_codes = jnp.where(slot_valid[:, :, None], codes[targets], -1).reshape(part_count, -1)
    own_codes = jnp.broadcast_to(codes.reshape(1, -1), (part_count, codes.size))
    lane_rows = 8
    room = -(-(codes.size + out_codes.shape[1]) // (lane_rows * 128)) * lane_rows * 128
    filler = jnp.zeros((part_count, room - codes.size - out_codes.shape[1]), jnp.int32)
    payload = jnp.concatenate([own_codes, out_codes, filler], axis=1)
    incoming = lax.all_to_all(
        payload.reshape(part_count, lane_rows, -1), "dom", 0, 0, tiled=True
    ).reshape(part_count, -1)
    recv_codes = incoming[:, codes.size : codes.size + out_codes.shape[1]].reshape(-1, book_count)
    hub_codes = [
        incoming[hub_owner[hub_index], : codes.size].reshape(codes.shape)
        for hub_index in range(NHUB)
    ]
    table_codes = jnp.concatenate([codes, recv_codes] + hub_codes, axis=0)
    table = decode(table_codes, complete_codebooks)
    local_rows = table[:rows_dev]
    blocks = table.reshape(-1, TB, model_width)
    tile_blocks = tiles.reshape(block_count, TPB, TB, TB)
    source_blocks = tile_src.reshape(block_count, TPB)
    relation_blocks = tile_rel.reshape(block_count, TPB)

    def forward_block(packed):
        weights_now, source_now, relation_now = packed
        composed = (
            blocks[source_now].astype(jnp.float32) * rel_table[relation_now][:, None, :]
        ).astype(jnp.bfloat16)
        summed = jnp.einsum(
            "tij,tjd->id", weights_now, composed, preferred_element_type=jnp.float32
        )
        return summed.astype(jnp.bfloat16)

    aggregate = lax.map(forward_block, (tile_blocks, source_blocks, relation_blocks)).reshape(
        rows_dev, model_width
    )
    pre_act = jnp.dot(aggregate, w_msg, preferred_element_type=jnp.float32) + jnp.dot(
        local_rows, w_self, preferred_element_type=jnp.float32
    )
    activated = jnp.tanh(pre_act)
    output = activated.astype(jnp.bfloat16)
    grad_pre = (cotangent.astype(jnp.float32) * (1.0 - activated * activated)).astype(jnp.bfloat16)
    contract_rows = (((0,), (0,)), ((), ()))
    contract_cols = (((1,), (1,)), ((), ()))
    grad_w_msg = lax.dot_general(
        aggregate, grad_pre, contract_rows, preferred_element_type=jnp.float32
    )
    grad_w_self = lax.dot_general(
        local_rows, grad_pre, contract_rows, preferred_element_type=jnp.float32
    )
    grad_agg = lax.dot_general(
        grad_pre, w_msg, contract_cols, preferred_element_type=jnp.float32
    ).astype(jnp.bfloat16)
    grad_self = lax.dot_general(grad_pre, w_self, contract_cols, preferred_element_type=jnp.float32)
    grad_blocks = grad_agg.reshape(block_count, TB, model_width)

    def backward_block(carry, packed):
        table_grad, rel_grad = carry
        weights_now, source_now, relation_now, upstream = packed
        grad_comp = jnp.einsum(
            "tji,jd->tid", weights_now, upstream, preferred_element_type=jnp.float32
        )
        rel_grad = rel_grad.at[relation_now].add(
            jnp.sum(grad_comp * blocks[source_now].astype(jnp.float32), axis=1)
        )
        table_grad = table_grad.at[source_now].add(grad_comp * rel_table[relation_now][:, None, :])
        return ((table_grad, rel_grad), None)

    start_carry = (jnp.zeros(blocks.shape, jnp.float32), jnp.zeros(rel_table.shape, jnp.float32))
    final_carry = lax.scan(
        backward_block, start_carry, (tile_blocks, source_blocks, relation_blocks, grad_blocks)
    )[0]
    table_grad, rel_grad = final_carry
    table_grad = table_grad.reshape(-1, model_width)
    table_grad = table_grad.at[:rows_dev].add(grad_self)
    book_grad = fold_books(table_codes, table_grad, code_count)
    part_alpha = jnp.dot(
        rel_grad, basis.T, precision=HIGHEST_PREC, preferred_element_type=jnp.float32
    )
    part_basis = jnp.dot(
        alpha.T, rel_grad, precision=HIGHEST_PREC, preferred_element_type=jnp.float32
    )
    total_msg, total_self, grad_basis, grad_alpha, grad_books = all_sum(
        grad_w_msg, grad_w_self, part_alpha, part_basis, book_grad, n_dom
    )
    return (output, total_msg, total_self, grad_alpha, grad_basis, grad_books)


def solution(mesh):
    n_dom = mesh.shape["dom"]

    def run(*args):
        return shards(n_dom, *args)

    return jax.shard_map(
        run,
        mesh=mesh,
        in_specs=(
            P(("dom", "sub"), None),
            P("sub", None, None),
            P(),
            P(),
            P(),
            P(),
            P(("dom", "sub"), None, None),
            P(("dom", "sub")),
            P(("dom", "sub")),
            P("dom", "sub", None, None),
            P("dom", "sub", None),
            P(),
            P(("dom", "sub"), None),
        ),
        out_specs=(P(("dom", "sub"), None), P(), P(), P(), P(), P("sub", None, None)),
        check_vma=False,
    )
```

```python
import jax
import jax.numpy as jnp
from jax import lax
from jax.sharding import PartitionSpec as P

TB = 128
TPB = 8
SLOT = 8
NHUB = 2


HIGHEST_PREC = lax.Precision.HIGHEST


def one_hot_codes(code_rows, code_count, out_type):
    return (code_rows[..., None] == jnp.arange(code_count, dtype=jnp.int32)).astype(out_type)


def decode(code_rows, complete_codebooks):
    indicator_rows = one_hot_codes(code_rows, complete_codebooks.shape[1], jnp.bfloat16)
    rows = jnp.einsum(
        "feu,euq->feq", indicator_rows, complete_codebooks, preferred_element_type=jnp.float32
    )
    return rows.astype(jnp.bfloat16).reshape(code_rows.shape[0], -1)


def fold_books(code_rows, gradients, code_count):
    book_count = code_rows.shape[1]
    indicator_rows = one_hot_codes(code_rows, code_count, jnp.bfloat16)
    pieces = gradients.reshape(gradients.shape[0], book_count, -1)
    upper_bound = pieces.astype(jnp.bfloat16)
    lower_bound = (pieces - upper_bound.astype(jnp.float32)).astype(jnp.bfloat16)
    upper_half_sum = jnp.einsum(
        "fco,fcg->cog", indicator_rows, upper_bound, preferred_element_type=jnp.float32
    )
    lower_half_sum = jnp.einsum(
        "fco,fcg->cog", indicator_rows, lower_bound, preferred_element_type=jnp.float32
    )
    return upper_half_sum + lower_half_sum


def all_sum(grad_w_msg, grad_w_self, part_alpha, part_basis, book_grad, n_dom):
    sub_index = lax.axis_index("sub")
    width = grad_w_msg.shape[1]
    share = book_grad.shape[0] // 2
    dense = [grad_w_msg, grad_w_self, part_basis, part_alpha.reshape(-1, width)]

    def half_of(h):
        pieces = [lax.dynamic_slice_in_dim(x, h * (x.shape[0] // 2), x.shape[0] // 2, 0) for x in dense]
        pieces.append(lax.dynamic_slice_in_dim(book_grad, h * share, share, 0).reshape(-1, width))
        return jnp.concatenate(pieces, axis=0)

    swap = [(0, 1), (1, 0)]
    mine = half_of(sub_index) + lax.ppermute(half_of(1 - sub_index), "sub", swap)
    rows = mine.shape[0]
    chunks = mine.astype(jnp.bfloat16).reshape(n_dom, -1, 128)
    received = lax.all_to_all(chunks, "dom", 0, 0, tiled=True)
    reduced = jnp.sum(received.astype(jnp.float32), axis=0).astype(jnp.bfloat16)
    spread = jnp.broadcast_to(reduced[None], chunks.shape)
    own_half = lax.all_to_all(spread, "dom", 0, 0, tiled=True).reshape(rows, width)
    dense_rows = rows - share * book_grad.shape[1] * book_grad.shape[2] // width
    own_dense = own_half[:dense_rows]
    other_dense = lax.ppermute(own_dense, "sub", swap)
    low = jnp.where(sub_index == 0, own_dense, other_dense).astype(jnp.float32)
    high = jnp.where(sub_index == 0, other_dense, own_dense).astype(jnp.float32)
    out = []
    start = 0
    for x in dense:
        r = x.shape[0] // 2
        out.append(jnp.concatenate([low[start : start + r], high[start : start + r]], axis=0))
        start += r
    out[3] = out[3].reshape(part_alpha.shape)
    books_mine = own_half[dense_rows:].astype(jnp.float32).reshape((share,) + book_grad.shape[1:])
    return out + [books_mine]


def shards(
    n_dom,
    codes,
    books,
    alpha,
    basis,
    w_msg,
    w_self,
    tiles,
    tile_src,
    tile_rel,
    send_rows,
    send_count,
    hub_owner,
    cotangent,
):
    rows_dev, book_count = codes.shape
    code_count = books.shape[1]
    model_width = w_msg.shape[0]
    tile_count = tiles.shape[0]
    block_count = tile_count // TPB
    complete_codebooks = lax.all_gather(books, "sub", axis=0, tiled=True)
    rel_table = jnp.dot(alpha, basis, precision=HIGHEST_PREC, preferred_element_type=jnp.float32)
    targets = send_rows[0, 0]
    part_count = targets.shape[0]
    slot_valid = jnp.arange(SLOT, dtype=jnp.int32)[None, :] < send_count[0, 0][:, None]
    out_codes = jnp.where(slot_valid[:, :, None], codes[targets], -1).reshape(part_count, -1)
    own_codes = jnp.broadcast_to(codes.reshape(1, -1), (part_count, codes.size))
    lane_rows = 8
    room = -(-(codes.size + out_codes.shape[1]) // (lane_rows * 128)) * lane_rows * 128
    filler = jnp.zeros((part_count, room - codes.size - out_codes.shape[1]), jnp.int32)
    payload = jnp.concatenate([own_codes, out_codes, filler], axis=1)
    incoming = lax.all_to_all(
        payload.reshape(part_count, lane_rows, -1), "dom", 0, 0, tiled=True
    ).reshape(part_count, -1)
    recv_codes = incoming[:, codes.size : codes.size + out_codes.shape[1]].reshape(-1, book_count)
    hub_codes = [
        incoming[hub_owner[hub_index], : codes.size].reshape(codes.shape)
        for hub_index in range(NHUB)
    ]
    table_codes = jnp.concatenate([codes, recv_codes] + hub_codes, axis=0)
    table = decode(table_codes, complete_codebooks)
    local_rows = table[:rows_dev]
    blocks = table.reshape(-1, TB, model_width)
    tile_blocks = tiles.reshape(block_count, TPB, TB, TB)
    picked = blocks[tile_src]
    scale = rel_table[tile_rel]
    composed = (picked.astype(jnp.float32) * scale[:, None, :]).astype(jnp.bfloat16)
    aggregate = jnp.einsum(
        "btij,btjd->bid",
        tile_blocks,
        composed.reshape(block_count, TPB, TB, model_width),
        preferred_element_type=jnp.float32,
    ).astype(jnp.bfloat16).reshape(rows_dev, model_width)
    pre_act = jnp.dot(aggregate, w_msg, preferred_element_type=jnp.float32) + jnp.dot(
        local_rows, w_self, preferred_element_type=jnp.float32
    )
    activated = jnp.tanh(pre_act)
    output = activated.astype(jnp.bfloat16)
    grad_pre = (cotangent.astype(jnp.float32) * (1.0 - activated * activated)).astype(jnp.bfloat16)
    contract_rows = (((0,), (0,)), ((), ()))
    contract_cols = (((1,), (1,)), ((), ()))
    grad_w_msg = lax.dot_general(
        aggregate, grad_pre, contract_rows, preferred_element_type=jnp.float32
    )
    grad_w_self = lax.dot_general(
        local_rows, grad_pre, contract_rows, preferred_element_type=jnp.float32
    )
    grad_agg = lax.dot_general(
        grad_pre, w_msg, contract_cols, preferred_element_type=jnp.float32
    ).astype(jnp.bfloat16)
    grad_self = lax.dot_general(grad_pre, w_self, contract_cols, preferred_element_type=jnp.float32)
    grad_blocks = grad_agg.reshape(block_count, TB, model_width)
    grad_comp = jnp.einsum(
        "btji,bjd->btid", tile_blocks, grad_blocks, preferred_element_type=jnp.float32
    ).reshape(tile_count, TB, model_width)
    rel_rows = jnp.sum(grad_comp * picked.astype(jnp.float32), axis=1)
    rel_grad = jnp.zeros(rel_table.shape, jnp.float32).at[tile_rel].add(rel_rows)
    table_grad = jnp.zeros(blocks.shape, jnp.float32).at[tile_src].add(
        grad_comp * scale[:, None, :]
    )
    table_grad = table_grad.reshape(-1, model_width)
    table_grad = table_grad.at[:rows_dev].add(grad_self)
    book_grad = fold_books(table_codes, table_grad, code_count)
    part_alpha = jnp.dot(
        rel_grad, basis.T, precision=HIGHEST_PREC, preferred_element_type=jnp.float32
    )
    part_basis = jnp.dot(
        alpha.T, rel_grad, precision=HIGHEST_PREC, preferred_element_type=jnp.float32
    )
    total_msg, total_self, grad_basis, grad_alpha, grad_books = all_sum(
        grad_w_msg, grad_w_self, part_alpha, part_basis, book_grad, n_dom
    )
    return (output, total_msg, total_self, grad_alpha, grad_basis, grad_books)


def solution(mesh):
    n_dom = mesh.shape["dom"]

    def run(*args):
        return shards(n_dom, *args)

    return jax.shard_map(
        run,
        mesh=mesh,
        in_specs=(
            P(("dom", "sub"), None),
            P("sub", None, None),
            P(),
            P(),
            P(),
            P(),
            P(("dom", "sub"), None, None),
            P(("dom", "sub")),
            P(("dom", "sub")),
            P("dom", "sub", None, None),
            P("dom", "sub", None),
            P(),
            P(("dom", "sub"), None),
        ),
        out_specs=(P(("dom", "sub"), None), P(), P(), P(), P(), P("sub", None, None)),
        check_vma=False,
    )
```

```python
import jax
import jax.numpy as jnp
from jax import lax
from jax.sharding import PartitionSpec as P

TB = 128
TPB = 8
SLOT = 8
NHUB = 2


HIGHEST_PREC = lax.Precision.HIGHEST


def one_hot_codes(code_rows, code_count, out_type):
    return (code_rows[..., None] == jnp.arange(code_count, dtype=jnp.int32)).astype(out_type)


def decode(code_rows, complete_codebooks):
    indicator_rows = one_hot_codes(code_rows, complete_codebooks.shape[1], jnp.bfloat16)
    rows = jnp.einsum(
        "feu,euq->feq", indicator_rows, complete_codebooks, preferred_element_type=jnp.float32
    )
    return rows.astype(jnp.bfloat16).reshape(code_rows.shape[0], -1)


def fold_books(code_rows, gradients, code_count):
    book_count = code_rows.shape[1]
    indicator_rows = one_hot_codes(code_rows, code_count, jnp.bfloat16)
    pieces = gradients.reshape(gradients.shape[0], book_count, -1)
    upper_bound = pieces.astype(jnp.bfloat16)
    lower_bound = (pieces - upper_bound.astype(jnp.float32)).astype(jnp.bfloat16)
    upper_half_sum = jnp.einsum(
        "fco,fcg->cog", indicator_rows, upper_bound, preferred_element_type=jnp.float32
    )
    lower_half_sum = jnp.einsum(
        "fco,fcg->cog", indicator_rows, lower_bound, preferred_element_type=jnp.float32
    )
    return upper_half_sum + lower_half_sum


def all_sum(grad_w_msg, grad_w_self, part_alpha, part_basis, book_grad, n_dom):
    sub_index = lax.axis_index("sub")
    width = grad_w_msg.shape[1]
    share = book_grad.shape[0] // 2
    dense = [grad_w_msg, grad_w_self, part_basis, part_alpha.reshape(-1, width)]

    def half_of(h):
        pieces = [lax.dynamic_slice_in_dim(x, h * (x.shape[0] // 2), x.shape[0] // 2, 0) for x in dense]
        pieces.append(lax.dynamic_slice_in_dim(book_grad, h * share, share, 0).reshape(-1, width))
        return jnp.concatenate(pieces, axis=0)

    swap = [(0, 1), (1, 0)]
    mine = half_of(sub_index) + lax.ppermute(half_of(1 - sub_index), "sub", swap)
    rows = mine.shape[0]
    chunks = mine.astype(jnp.bfloat16).reshape(n_dom, -1, 128)
    received = lax.all_to_all(chunks, "dom", 0, 0, tiled=True)
    reduced = jnp.sum(received.astype(jnp.float32), axis=0).astype(jnp.bfloat16)
    spread = jnp.broadcast_to(reduced[None], chunks.shape)
    own_half = lax.all_to_all(spread, "dom", 0, 0, tiled=True).reshape(rows, width)
    dense_rows = rows - share * book_grad.shape[1] * book_grad.shape[2] // width
    own_dense = own_half[:dense_rows]
    other_dense = lax.ppermute(own_dense, "sub", swap)
    low = jnp.where(sub_index == 0, own_dense, other_dense).astype(jnp.float32)
    high = jnp.where(sub_index == 0, other_dense, own_dense).astype(jnp.float32)
    out = []
    start = 0
    for x in dense:
        r = x.shape[0] // 2
        out.append(jnp.concatenate([low[start : start + r], high[start : start + r]], axis=0))
        start += r
    out[3] = out[3].reshape(part_alpha.shape)
    books_mine = own_half[dense_rows:].astype(jnp.float32).reshape((share,) + book_grad.shape[1:])
    return out + [books_mine]


def shards(
    n_dom,
    codes,
    books,
    alpha,
    basis,
    w_msg,
    w_self,
    tiles,
    tile_src,
    tile_rel,
    send_rows,
    send_count,
    hub_owner,
    cotangent,
):
    rows_dev, book_count = codes.shape
    code_count = books.shape[1]
    model_width = w_msg.shape[0]
    tile_count = tiles.shape[0]
    block_count = tile_count // TPB
    complete_codebooks = lax.all_gather(books, "sub", axis=0, tiled=True)
    rel_table = jnp.dot(alpha, basis, precision=HIGHEST_PREC, preferred_element_type=jnp.float32)
    targets = send_rows[0, 0]
    part_count = targets.shape[0]
    slot_valid = jnp.arange(SLOT, dtype=jnp.int32)[None, :] < send_count[0, 0][:, None]
    out_codes = jnp.where(slot_valid[:, :, None], codes[targets], -1).reshape(part_count, -1)
    own_codes = jnp.broadcast_to(codes.reshape(1, -1), (part_count, codes.size))
    room = -(-(codes.size + out_codes.shape[1]) // 128) * 128
    filler = jnp.zeros((part_count, room - codes.size - out_codes.shape[1]), jnp.int32)
    payload = jnp.concatenate([own_codes, out_codes, filler], axis=1)
    incoming = lax.all_to_all(payload, "dom", 0, 0, tiled=True)
    recv_codes = incoming[:, codes.size : codes.size + out_codes.shape[1]].reshape(-1, book_count)
    hub_codes = [
        incoming[hub_owner[hub_index], : codes.size].reshape(codes.shape)
        for hub_index in range(NHUB)
    ]
    table_codes = jnp.concatenate([codes, recv_codes] + hub_codes, axis=0)
    table = decode(table_codes, complete_codebooks)
    local_rows = table[:rows_dev]
    blocks = table.reshape(-1, TB, model_width)
    tile_blocks = tiles.reshape(block_count, TPB, TB, TB)
    picked = blocks[tile_src]
    scale = rel_table[tile_rel]
    composed = (picked.astype(jnp.float32) * scale[:, None, :]).astype(jnp.bfloat16)
    aggregate = jnp.einsum(
        "btij,btjd->bid",
        tile_blocks,
        composed.reshape(block_count, TPB, TB, model_width),
        preferred_element_type=jnp.float32,
    ).astype(jnp.bfloat16).reshape(rows_dev, model_width)
    pre_act = jnp.dot(aggregate, w_msg, preferred_element_type=jnp.float32) + jnp.dot(
        local_rows, w_self, preferred_element_type=jnp.float32
    )
    activated = jnp.tanh(pre_act)
    output = activated.astype(jnp.bfloat16)
    grad_pre = (cotangent.astype(jnp.float32) * (1.0 - activated * activated)).astype(jnp.bfloat16)
    contract_rows = (((0,), (0,)), ((), ()))
    contract_cols = (((1,), (1,)), ((), ()))
    grad_w_msg = lax.dot_general(
        aggregate, grad_pre, contract_rows, preferred_element_type=jnp.float32
    )
    grad_w_self = lax.dot_general(
        local_rows, grad_pre, contract_rows, preferred_element_type=jnp.float32
    )
    grad_agg = lax.dot_general(
        grad_pre, w_msg, contract_cols, preferred_element_type=jnp.float32
    ).astype(jnp.bfloat16)
    grad_self = lax.dot_general(grad_pre, w_self, contract_cols, preferred_element_type=jnp.float32)
    grad_blocks = grad_agg.reshape(block_count, TB, model_width)
    grad_comp = jnp.einsum(
        "btji,bjd->btid", tile_blocks, grad_blocks, preferred_element_type=jnp.float32
    ).reshape(tile_count, TB, model_width)
    rel_rows = jnp.sum(grad_comp * picked.astype(jnp.float32), axis=1)
    rel_grad = jnp.zeros(rel_table.shape, jnp.float32).at[tile_rel].add(rel_rows)
    src_hot = one_hot_codes(tile_src, blocks.shape[0], jnp.float32)
    table_grad = jnp.einsum(
        "ts,tjd->sjd",
        src_hot,
        grad_comp * scale[:, None, :],
        precision=HIGHEST_PREC,
        preferred_element_type=jnp.float32,
    )
    table_grad = table_grad.reshape(-1, model_width)
    table_grad = table_grad.at[:rows_dev].add(grad_self)
    book_grad = fold_books(table_codes, table_grad, code_count)
    part_alpha = jnp.dot(
        rel_grad, basis.T, precision=HIGHEST_PREC, preferred_element_type=jnp.float32
    )
    part_basis = jnp.dot(
        alpha.T, rel_grad, precision=HIGHEST_PREC, preferred_element_type=jnp.float32
    )
    total_msg, total_self, grad_basis, grad_alpha, grad_books = all_sum(
        grad_w_msg, grad_w_self, part_alpha, part_basis, book_grad, n_dom
    )
    return (output, total_msg, total_self, grad_alpha, grad_basis, grad_books)


def solution(mesh):
    n_dom = mesh.shape["dom"]

    def run(*args):
        return shards(n_dom, *args)

    return jax.shard_map(
        run,
        mesh=mesh,
        in_specs=(
            P(("dom", "sub"), None),
            P("sub", None, None),
            P(),
            P(),
            P(),
            P(),
            P(("dom", "sub"), None, None),
            P(("dom", "sub")),
            P(("dom", "sub")),
            P("dom", "sub", None, None),
            P("dom", "sub", None),
            P(),
            P(("dom", "sub"), None),
        ),
        out_specs=(P(("dom", "sub"), None), P(), P(), P(), P(), P("sub", None, None)),
        check_vma=False,
    )
```

```python
import jax
import jax.numpy as jnp
from jax import lax
from jax.sharding import Mesh, PartitionSpec as P
import numpy as np

TB = 128
TPB = 8
SLOT = 8
NHUB = 2
DOM = ("dy", "dx", "dz")


HIGHEST_PREC = lax.Precision.HIGHEST


def one_hot_codes(code_rows, code_count, out_type):
    return (code_rows[..., None] == jnp.arange(code_count, dtype=jnp.int32)).astype(out_type)


def decode(code_rows, complete_codebooks):
    indicator_rows = one_hot_codes(code_rows, complete_codebooks.shape[1], jnp.bfloat16)
    rows = jnp.einsum(
        "feu,euq->feq", indicator_rows, complete_codebooks, preferred_element_type=jnp.float32
    )
    return rows.astype(jnp.bfloat16).reshape(code_rows.shape[0], -1)


def fold_books(code_rows, gradients, code_count):
    book_count = code_rows.shape[1]
    indicator_rows = one_hot_codes(code_rows, code_count, jnp.bfloat16)
    pieces = gradients.reshape(gradients.shape[0], book_count, -1)
    upper_bound = pieces.astype(jnp.bfloat16)
    lower_bound = (pieces - upper_bound.astype(jnp.float32)).astype(jnp.bfloat16)
    upper_half_sum = jnp.einsum(
        "fco,fcg->cog", indicator_rows, upper_bound, preferred_element_type=jnp.float32
    )
    lower_half_sum = jnp.einsum(
        "fco,fcg->cog", indicator_rows, lower_bound, preferred_element_type=jnp.float32
    )
    return upper_half_sum + lower_half_sum


def all_sum(grad_w_msg, grad_w_self, part_alpha, part_basis, book_grad, dom_axes):
    sub_index = lax.axis_index("sub")
    width = grad_w_msg.shape[1]
    share = book_grad.shape[0] // 2
    dense = [grad_w_msg, grad_w_self, part_basis, part_alpha.reshape(-1, width)]

    def half_of(h):
        pieces = [lax.dynamic_slice_in_dim(x, h * (x.shape[0] // 2), x.shape[0] // 2, 0) for x in dense]
        pieces.append(lax.dynamic_slice_in_dim(book_grad, h * share, share, 0).reshape(-1, width))
        return jnp.concatenate(pieces, axis=0)

    swap = [(0, 1), (1, 0)]
    mine = half_of(sub_index) + lax.ppermute(half_of(1 - sub_index), "sub", swap)
    rows = mine.shape[0]
    shapes = []
    piece = mine
    for stage, (axis, size) in enumerate(dom_axes):
        shapes.append(piece.shape)
        lanes = piece.shape[-1]
        if piece.shape[0] % size:
            lanes = 256
        chunks = piece.reshape(size, -1, lanes)
        if stage == 0:
            chunks = chunks.astype(jnp.bfloat16)
        received = lax.all_to_all(chunks, axis, 0, 0, tiled=True)
        piece = jnp.sum(received.astype(jnp.float32), axis=0)
    piece = piece.astype(jnp.bfloat16)
    for (axis, size), shape in reversed(list(zip(dom_axes, shapes))):
        spread = jnp.broadcast_to(piece[None], (size,) + piece.shape)
        piece = lax.all_to_all(spread, axis, 0, 0, tiled=True).reshape(shape)
    own_half = piece
    dense_rows = rows - share * book_grad.shape[1] * book_grad.shape[2] // width
    own_dense = own_half[:dense_rows]
    other_dense = lax.ppermute(own_dense, "sub", swap)
    low = jnp.where(sub_index == 0, own_dense, other_dense).astype(jnp.float32)
    high = jnp.where(sub_index == 0, other_dense, own_dense).astype(jnp.float32)
    out = []
    start = 0
    for x in dense:
        r = x.shape[0] // 2
        out.append(jnp.concatenate([low[start : start + r], high[start : start + r]], axis=0))
        start += r
    out[3] = out[3].reshape(part_alpha.shape)
    books_mine = own_half[dense_rows:].astype(jnp.float32).reshape((share,) + book_grad.shape[1:])
    return out + [books_mine]


def shards(
    dom_axes,
    codes,
    books,
    alpha,
    basis,
    w_msg,
    w_self,
    tiles,
    tile_src,
    tile_rel,
    send_rows,
    send_count,
    hub_owner,
    cotangent,
):
    rows_dev, book_count = codes.shape
    code_count = books.shape[1]
    model_width = w_msg.shape[0]
    tile_count = tiles.shape[0]
    block_count = tile_count // TPB
    complete_codebooks = lax.all_gather(books, "sub", axis=0, tiled=True)
    rel_table = jnp.dot(alpha, basis, precision=HIGHEST_PREC, preferred_element_type=jnp.float32)
    targets = send_rows[0, 0]
    part_count = targets.shape[0]
    slot_valid = jnp.arange(SLOT, dtype=jnp.int32)[None, :] < send_count[0, 0][:, None]
    out_codes = jnp.where(slot_valid[:, :, None], codes[targets], -1).reshape(part_count, -1)
    own_codes = jnp.broadcast_to(codes.reshape(1, -1), (part_count, codes.size))
    room = -(-(codes.size + out_codes.shape[1]) // 128) * 128
    filler = jnp.zeros((part_count, room - codes.size - out_codes.shape[1]), jnp.int32)
    payload = jnp.concatenate([own_codes, out_codes, filler], axis=1)
    incoming = lax.all_to_all(payload, DOM, 0, 0, tiled=True)
    recv_codes = incoming[:, codes.size : codes.size + out_codes.shape[1]].reshape(-1, book_count)
    hub_codes = [
        incoming[hub_owner[hub_index], : codes.size].reshape(codes.shape)
        for hub_index in range(NHUB)
    ]
    table_codes = jnp.concatenate([codes, recv_codes] + hub_codes, axis=0)
    table = decode(table_codes, complete_codebooks)
    local_rows = table[:rows_dev]
    blocks = table.reshape(-1, TB, model_width)
    tile_blocks = tiles.reshape(block_count, TPB, TB, TB)
    picked = blocks[tile_src]
    scale = rel_table[tile_rel]
    composed = (picked.astype(jnp.float32) * scale[:, None, :]).astype(jnp.bfloat16)
    aggregate = jnp.einsum(
        "btij,btjd->bid",
        tile_blocks,
        composed.reshape(block_count, TPB, TB, model_width),
        preferred_element_type=jnp.float32,
    ).astype(jnp.bfloat16).reshape(rows_dev, model_width)
    pre_act = jnp.dot(aggregate, w_msg, preferred_element_type=jnp.float32) + jnp.dot(
        local_rows, w_self, preferred_element_type=jnp.float32
    )
    activated = jnp.tanh(pre_act)
    output = activated.astype(jnp.bfloat16)
    grad_pre = (cotangent.astype(jnp.float32) * (1.0 - activated * activated)).astype(jnp.bfloat16)
    contract_rows = (((0,), (0,)), ((), ()))
    contract_cols = (((1,), (1,)), ((), ()))
    grad_w_msg = lax.dot_general(
        aggregate, grad_pre, contract_rows, preferred_element_type=jnp.float32
    )
    grad_w_self = lax.dot_general(
        local_rows, grad_pre, contract_rows, preferred_element_type=jnp.float32
    )
    grad_agg = lax.dot_general(
        grad_pre, w_msg, contract_cols, preferred_element_type=jnp.float32
    ).astype(jnp.bfloat16)
    grad_self = lax.dot_general(grad_pre, w_self, contract_cols, preferred_element_type=jnp.float32)
    grad_blocks = grad_agg.reshape(block_count, TB, model_width)
    grad_comp = jnp.einsum(
        "btji,bjd->btid", tile_blocks, grad_blocks, preferred_element_type=jnp.float32
    ).reshape(tile_count, TB, model_width)
    rel_rows = jnp.sum(grad_comp * picked.astype(jnp.float32), axis=1)
    rel_grad = jnp.zeros(rel_table.shape, jnp.float32).at[tile_rel].add(rel_rows)
    src_hot = one_hot_codes(tile_src, blocks.shape[0], jnp.float32)
    table_grad = jnp.einsum(
        "ts,tjd->sjd",
        src_hot,
        grad_comp * scale[:, None, :],
        precision=HIGHEST_PREC,
        preferred_element_type=jnp.float32,
    )
    table_grad = table_grad.reshape(-1, model_width)
    table_grad = table_grad.at[:rows_dev].add(grad_self)
    book_grad = fold_books(table_codes, table_grad, code_count)
    part_alpha = jnp.dot(
        rel_grad, basis.T, precision=HIGHEST_PREC, preferred_element_type=jnp.float32
    )
    part_basis = jnp.dot(
        alpha.T, rel_grad, precision=HIGHEST_PREC, preferred_element_type=jnp.float32
    )
    total_msg, total_self, grad_basis, grad_alpha, grad_books = all_sum(
        grad_w_msg, grad_w_self, part_alpha, part_basis, book_grad, dom_axes
    )
    return (output, total_msg, total_self, grad_alpha, grad_basis, grad_books)


def split_mesh(mesh):
    grid = np.asarray(mesh.devices)
    try:
        coords = np.array([d.coords for d in grid.reshape(-1)]).reshape(grid.shape + (-1,))
    except (AttributeError, ValueError):
        return None
    ny, nx, nz = (len(np.unique(coords[..., k])) for k in (1, 0, 2))
    if ny * nx * nz != grid.shape[0]:
        return None
    cube = coords.reshape(ny, nx, nz, grid.shape[1], -1)
    for axis, k in ((0, 1), (1, 0), (2, 2)):
        others = [c for c in range(3) if c != k]
        if np.any(np.diff(cube[..., others], axis=axis) != 0):
            return None
    return Mesh(grid.reshape(ny, nx, nz, grid.shape[1]), DOM + ("sub",)), (ny, nx, nz)


def solution(mesh):
    found = split_mesh(mesh)
    assert found is not None
    fine_mesh, (ny, nx, nz) = found
    dom_axes = (("dx", nx), ("dy", ny), ("dz", nz))

    def run(*args):
        return shards(dom_axes, *args)

    rows = P(DOM + ("sub",))
    return jax.shard_map(
        run,
        mesh=fine_mesh,
        in_specs=(
            P(DOM + ("sub",), None),
            P("sub", None, None),
            P(),
            P(),
            P(),
            P(),
            P(DOM + ("sub",), None, None),
            rows,
            rows,
            P(DOM, "sub", None, None),
            P(DOM, "sub", None),
            P(),
            P(DOM + ("sub",), None),
        ),
        out_specs=(P(DOM + ("sub",), None), P(), P(), P(), P(), P("sub", None, None)),
        check_vma=False,
    )
```

```python
import jax
import jax.numpy as jnp
from jax import lax
from jax.sharding import PartitionSpec as P

TB = 128
TPB = 8
SLOT = 8
NHUB = 2


HIGHEST_PREC = lax.Precision.HIGHEST


def one_hot_codes(code_rows, code_count, out_type):
    return (code_rows[..., None] == jnp.arange(code_count, dtype=jnp.int32)).astype(out_type)


def decode(code_rows, complete_codebooks):
    indicator_rows = one_hot_codes(code_rows, complete_codebooks.shape[1], jnp.bfloat16)
    rows = jnp.einsum(
        "feu,euq->feq", indicator_rows, complete_codebooks, preferred_element_type=jnp.float32
    )
    return rows.astype(jnp.bfloat16).reshape(code_rows.shape[0], -1)


def fold_books(code_rows, gradients, code_count):
    book_count = code_rows.shape[1]
    indicator_rows = one_hot_codes(code_rows, code_count, jnp.bfloat16)
    pieces = gradients.reshape(gradients.shape[0], book_count, -1)
    upper_bound = pieces.astype(jnp.bfloat16)
    lower_bound = (pieces - upper_bound.astype(jnp.float32)).astype(jnp.bfloat16)
    upper_half_sum = jnp.einsum(
        "fco,fcg->cog", indicator_rows, upper_bound, preferred_element_type=jnp.float32
    )
    lower_half_sum = jnp.einsum(
        "fco,fcg->cog", indicator_rows, lower_bound, preferred_element_type=jnp.float32
    )
    return upper_half_sum + lower_half_sum


def all_sum(grad_w_msg, grad_w_self, part_alpha, part_basis, book_grad, n_dom):
    sub_index = lax.axis_index("sub")
    width = grad_w_msg.shape[1]
    share = book_grad.shape[0] // 2
    dense = [grad_w_msg, grad_w_self, part_basis, part_alpha.reshape(-1, width)]

    def half_of(h):
        pieces = [lax.dynamic_slice_in_dim(x, h * (x.shape[0] // 2), x.shape[0] // 2, 0) for x in dense]
        pieces.append(lax.dynamic_slice_in_dim(book_grad, h * share, share, 0).reshape(-1, width))
        return jnp.concatenate(pieces, axis=0)

    swap = [(0, 1), (1, 0)]
    mine = half_of(sub_index) + lax.ppermute(half_of(1 - sub_index), "sub", swap)
    rows = mine.shape[0]
    chunks = mine.astype(jnp.bfloat16).reshape(n_dom, -1)
    received = lax.all_to_all(chunks, "dom", 0, 0, tiled=True)
    reduced = jnp.sum(received.astype(jnp.float32), axis=0).astype(jnp.bfloat16)
    spread = jnp.broadcast_to(reduced[None], chunks.shape)
    own_half = lax.all_to_all(spread, "dom", 0, 0, tiled=True).reshape(rows, width)
    dense_rows = rows - share * book_grad.shape[1] * book_grad.shape[2] // width
    own_dense = own_half[:dense_rows]
    other_dense = lax.ppermute(own_dense, "sub", swap)
    low = jnp.where(sub_index == 0, own_dense, other_dense).astype(jnp.float32)
    high = jnp.where(sub_index == 0, other_dense, own_dense).astype(jnp.float32)
    out = []
    start = 0
    for x in dense:
        r = x.shape[0] // 2
        out.append(jnp.concatenate([low[start : start + r], high[start : start + r]], axis=0))
        start += r
    out[3] = out[3].reshape(part_alpha.shape)
    books_mine = own_half[dense_rows:].astype(jnp.float32).reshape((share,) + book_grad.shape[1:])
    return out + [books_mine]


def shards(
    n_dom,
    codes,
    books,
    alpha,
    basis,
    w_msg,
    w_self,
    tiles,
    tile_src,
    tile_rel,
    send_rows,
    send_count,
    hub_owner,
    cotangent,
):
    rows_dev, book_count = codes.shape
    code_count = books.shape[1]
    model_width = w_msg.shape[0]
    tile_count = tiles.shape[0]
    block_count = tile_count // TPB
    complete_codebooks = lax.all_gather(books, "sub", axis=0, tiled=True)
    rel_table = jnp.dot(alpha, basis, precision=HIGHEST_PREC, preferred_element_type=jnp.float32)
    targets = send_rows[0, 0]
    part_count = targets.shape[0]
    slot_valid = jnp.arange(SLOT, dtype=jnp.int32)[None, :] < send_count[0, 0][:, None]
    out_codes = jnp.where(slot_valid[:, :, None], codes[targets], -1).reshape(part_count, -1)
    own_codes = jnp.broadcast_to(codes.reshape(1, -1), (part_count, codes.size))
    room = -(-(codes.size + out_codes.shape[1]) // 128) * 128
    filler = jnp.zeros((part_count, room - codes.size - out_codes.shape[1]), jnp.int32)
    payload = jnp.concatenate([own_codes, out_codes, filler], axis=1).astype(jnp.int16)
    incoming = lax.all_to_all(payload, "dom", 0, 0, tiled=True).astype(jnp.int32)
    recv_codes = incoming[:, codes.size : codes.size + out_codes.shape[1]].reshape(-1, book_count)
    hub_codes = [
        incoming[hub_owner[hub_index], : codes.size].reshape(codes.shape)
        for hub_index in range(NHUB)
    ]
    table_codes = jnp.concatenate([codes, recv_codes] + hub_codes, axis=0)
    table = decode(table_codes, complete_codebooks)
    local_rows = table[:rows_dev]
    blocks = table.reshape(-1, TB, model_width)
    tile_blocks = tiles.reshape(block_count, TPB, TB, TB)
    picked = blocks[tile_src]
    scale = rel_table[tile_rel]
    composed = (picked.astype(jnp.float32) * scale[:, None, :]).astype(jnp.bfloat16)
    aggregate = jnp.einsum(
        "btij,btjd->bid",
        tile_blocks,
        composed.reshape(block_count, TPB, TB, model_width),
        preferred_element_type=jnp.float32,
    ).astype(jnp.bfloat16).reshape(rows_dev, model_width)
    pre_act = jnp.dot(aggregate, w_msg, preferred_element_type=jnp.float32) + jnp.dot(
        local_rows, w_self, preferred_element_type=jnp.float32
    )
    activated = jnp.tanh(pre_act)
    output = activated.astype(jnp.bfloat16)
    grad_pre = (cotangent.astype(jnp.float32) * (1.0 - activated * activated)).astype(jnp.bfloat16)
    contract_rows = (((0,), (0,)), ((), ()))
    contract_cols = (((1,), (1,)), ((), ()))
    grad_w_msg = lax.dot_general(
        aggregate, grad_pre, contract_rows, preferred_element_type=jnp.float32
    )
    grad_w_self = lax.dot_general(
        local_rows, grad_pre, contract_rows, preferred_element_type=jnp.float32
    )
    grad_agg = lax.dot_general(
        grad_pre, w_msg, contract_cols, preferred_element_type=jnp.float32
    ).astype(jnp.bfloat16)
    grad_self = lax.dot_general(grad_pre, w_self, contract_cols, preferred_element_type=jnp.float32)
    grad_blocks = grad_agg.reshape(block_count, TB, model_width)
    grad_comp = jnp.einsum(
        "btji,bjd->btid", tile_blocks, grad_blocks, preferred_element_type=jnp.float32
    ).reshape(tile_count, TB, model_width)
    rel_rows = jnp.sum(grad_comp * picked.astype(jnp.float32), axis=1)
    rel_grad = jnp.zeros(rel_table.shape, jnp.float32).at[tile_rel].add(rel_rows)
    src_hot = one_hot_codes(tile_src, blocks.shape[0], jnp.float32)
    table_grad = jnp.einsum(
        "ts,tjd->sjd",
        src_hot,
        grad_comp * scale[:, None, :],
        precision=HIGHEST_PREC,
        preferred_element_type=jnp.float32,
    )
    table_grad = table_grad.reshape(-1, model_width)
    table_grad = table_grad.at[:rows_dev].add(grad_self)
    book_grad = fold_books(table_codes, table_grad, code_count)
    part_alpha = jnp.dot(
        rel_grad, basis.T, precision=HIGHEST_PREC, preferred_element_type=jnp.float32
    )
    part_basis = jnp.dot(
        alpha.T, rel_grad, precision=HIGHEST_PREC, preferred_element_type=jnp.float32
    )
    total_msg, total_self, grad_basis, grad_alpha, grad_books = all_sum(
        grad_w_msg, grad_w_self, part_alpha, part_basis, book_grad, n_dom
    )
    return (output, total_msg, total_self, grad_alpha, grad_basis, grad_books)


def solution(mesh):
    n_dom = mesh.shape["dom"]

    def run(*args):
        return shards(n_dom, *args)

    return jax.shard_map(
        run,
        mesh=mesh,
        in_specs=(
            P(("dom", "sub"), None),
            P("sub", None, None),
            P(),
            P(),
            P(),
            P(),
            P(("dom", "sub"), None, None),
            P(("dom", "sub")),
            P(("dom", "sub")),
            P("dom", "sub", None, None),
            P("dom", "sub", None),
            P(),
            P(("dom", "sub"), None),
        ),
        out_specs=(P(("dom", "sub"), None), P(), P(), P(), P(), P("sub", None, None)),
        check_vma=False,
    )
```

```python
import jax
import jax.numpy as jnp
from jax import lax
from jax.sharding import PartitionSpec as P

TB = 128
TPB = 8
SLOT = 8
NHUB = 2


HIGHEST_PREC = lax.Precision.HIGHEST


def one_hot_codes(code_rows, code_count, out_type):
    return (code_rows[..., None] == jnp.arange(code_count, dtype=jnp.int32)).astype(out_type)


def decode(code_rows, complete_codebooks):
    indicator_rows = one_hot_codes(code_rows, complete_codebooks.shape[1], jnp.bfloat16)
    rows = jnp.einsum(
        "feu,euq->feq", indicator_rows, complete_codebooks, preferred_element_type=jnp.float32
    )
    return rows.astype(jnp.bfloat16).reshape(code_rows.shape[0], -1)


def fold_books(code_rows, gradients, code_count):
    book_count = code_rows.shape[1]
    indicator_rows = one_hot_codes(code_rows, code_count, jnp.bfloat16)
    pieces = gradients.reshape(gradients.shape[0], book_count, -1)
    upper_bound = pieces.astype(jnp.bfloat16)
    lower_bound = (pieces - upper_bound.astype(jnp.float32)).astype(jnp.bfloat16)
    upper_half_sum = jnp.einsum(
        "fco,fcg->cog", indicator_rows, upper_bound, preferred_element_type=jnp.float32
    )
    lower_half_sum = jnp.einsum(
        "fco,fcg->cog", indicator_rows, lower_bound, preferred_element_type=jnp.float32
    )
    return upper_half_sum + lower_half_sum


def all_sum(grad_w_msg, grad_w_self, part_alpha, part_basis, book_grad, n_dom):
    sub_index = lax.axis_index("sub")
    width = grad_w_msg.shape[1]
    share = book_grad.shape[0] // 2
    dense = [grad_w_msg, grad_w_self, part_basis, part_alpha.reshape(-1, width)]

    def half_of(h):
        pieces = [lax.dynamic_slice_in_dim(x, h * (x.shape[0] // 2), x.shape[0] // 2, 0) for x in dense]
        pieces.append(lax.dynamic_slice_in_dim(book_grad, h * share, share, 0).reshape(-1, width))
        return jnp.concatenate(pieces, axis=0)

    swap = [(0, 1), (1, 0)]
    mine = half_of(sub_index) + lax.ppermute(half_of(1 - sub_index), "sub", swap)
    rows = mine.shape[0]
    chunks = mine.astype(jnp.bfloat16).reshape(n_dom, -1, 128)
    received = lax.all_to_all(chunks, "dom", 0, 0, tiled=True)
    reduced = jnp.sum(received.astype(jnp.float32), axis=0).astype(jnp.bfloat16)
    spread = jnp.broadcast_to(reduced[None], chunks.shape)
    own_half = lax.all_to_all(spread, "dom", 0, 0, tiled=True).reshape(rows, width)
    dense_rows = rows - share * book_grad.shape[1] * book_grad.shape[2] // width
    own_dense = own_half[:dense_rows]
    other_dense = lax.ppermute(own_dense, "sub", swap)
    low = jnp.where(sub_index == 0, own_dense, other_dense).astype(jnp.float32)
    high = jnp.where(sub_index == 0, other_dense, own_dense).astype(jnp.float32)
    out = []
    start = 0
    for x in dense:
        r = x.shape[0] // 2
        out.append(jnp.concatenate([low[start : start + r], high[start : start + r]], axis=0))
        start += r
    out[3] = out[3].reshape(part_alpha.shape)
    books_mine = own_half[dense_rows:].astype(jnp.float32).reshape((share,) + book_grad.shape[1:])
    return out + [books_mine]


def shards(
    n_dom,
    codes,
    books,
    alpha,
    basis,
    w_msg,
    w_self,
    tiles,
    tile_src,
    tile_rel,
    send_rows,
    send_count,
    hub_owner,
    cotangent,
):
    rows_dev, book_count = codes.shape
    code_count = books.shape[1]
    model_width = w_msg.shape[0]
    tile_count = tiles.shape[0]
    block_count = tile_count // TPB
    complete_codebooks = lax.all_gather(books, "sub", axis=0, tiled=True)
    rel_table = jnp.dot(alpha, basis, precision=HIGHEST_PREC, preferred_element_type=jnp.float32)
    targets = send_rows[0, 0]
    part_count = targets.shape[0]
    slot_valid = jnp.arange(SLOT, dtype=jnp.int32)[None, :] < send_count[0, 0][:, None]
    out_codes = jnp.where(slot_valid[:, :, None], codes[targets], -1).reshape(part_count, -1)
    own_codes = jnp.broadcast_to(codes.reshape(1, -1), (part_count, codes.size))
    room = -(-(codes.size + out_codes.shape[1]) // 128) * 128
    filler = jnp.zeros((part_count, room - codes.size - out_codes.shape[1]), jnp.int32)
    payload = jnp.concatenate([own_codes, out_codes, filler], axis=1)
    incoming = lax.all_to_all(payload, "dom", 0, 0, tiled=True)
    recv_codes = incoming[:, codes.size : codes.size + out_codes.shape[1]].reshape(-1, book_count)
    hub_codes = [
        incoming[hub_owner[hub_index], : codes.size].reshape(codes.shape)
        for hub_index in range(NHUB)
    ]
    table_codes = jnp.concatenate([codes, recv_codes] + hub_codes, axis=0)
    local_rows = decode(codes, complete_codebooks)
    table = jnp.concatenate(
        [local_rows, decode(table_codes[rows_dev:], complete_codebooks)], axis=0
    )
    blocks = table.reshape(-1, TB, model_width)
    tile_blocks = tiles.reshape(block_count, TPB, TB, TB)
    picked = blocks[tile_src]
    scale = rel_table[tile_rel]
    composed = (picked.astype(jnp.float32) * scale[:, None, :]).astype(jnp.bfloat16)
    aggregate = jnp.einsum(
        "btij,btjd->bid",
        tile_blocks,
        composed.reshape(block_count, TPB, TB, model_width),
        preferred_element_type=jnp.float32,
    ).astype(jnp.bfloat16).reshape(rows_dev, model_width)
    pre_act = jnp.dot(aggregate, w_msg, preferred_element_type=jnp.float32) + jnp.dot(
        local_rows, w_self, preferred_element_type=jnp.float32
    )
    activated = jnp.tanh(pre_act)
    output = activated.astype(jnp.bfloat16)
    grad_pre = (cotangent.astype(jnp.float32) * (1.0 - activated * activated)).astype(jnp.bfloat16)
    contract_rows = (((0,), (0,)), ((), ()))
    contract_cols = (((1,), (1,)), ((), ()))
    grad_w_msg = lax.dot_general(
        aggregate, grad_pre, contract_rows, preferred_element_type=jnp.float32
    )
    grad_w_self = lax.dot_general(
        local_rows, grad_pre, contract_rows, preferred_element_type=jnp.float32
    )
    grad_agg = lax.dot_general(
        grad_pre, w_msg, contract_cols, preferred_element_type=jnp.float32
    ).astype(jnp.bfloat16)
    grad_self = lax.dot_general(grad_pre, w_self, contract_cols, preferred_element_type=jnp.float32)
    grad_blocks = grad_agg.reshape(block_count, TB, model_width)
    grad_comp = jnp.einsum(
        "btji,bjd->btid", tile_blocks, grad_blocks, preferred_element_type=jnp.float32
    ).reshape(tile_count, TB, model_width)
    rel_rows = jnp.sum(grad_comp * picked.astype(jnp.float32), axis=1)
    rel_grad = jnp.zeros(rel_table.shape, jnp.float32).at[tile_rel].add(rel_rows)
    tile_codes = table_codes.reshape(-1, TB, book_count)[tile_src].reshape(-1, book_count)
    contrib = (grad_comp * scale[:, None, :]).reshape(-1, model_width)
    book_grad = fold_books(tile_codes, contrib, code_count) + fold_books(codes, grad_self, code_count)
    part_alpha = jnp.dot(
        rel_grad, basis.T, precision=HIGHEST_PREC, preferred_element_type=jnp.float32
    )
    part_basis = jnp.dot(
        alpha.T, rel_grad, precision=HIGHEST_PREC, preferred_element_type=jnp.float32
    )
    total_msg, total_self, grad_basis, grad_alpha, grad_books = all_sum(
        grad_w_msg, grad_w_self, part_alpha, part_basis, book_grad, n_dom
    )
    return (output, total_msg, total_self, grad_alpha, grad_basis, grad_books)


def solution(mesh):
    n_dom = mesh.shape["dom"]

    def run(*args):
        return shards(n_dom, *args)

    return jax.shard_map(
        run,
        mesh=mesh,
        in_specs=(
            P(("dom", "sub"), None),
            P("sub", None, None),
            P(),
            P(),
            P(),
            P(),
            P(("dom", "sub"), None, None),
            P(("dom", "sub")),
            P(("dom", "sub")),
            P("dom", "sub", None, None),
            P("dom", "sub", None),
            P(),
            P(("dom", "sub"), None),
        ),
        out_specs=(P(("dom", "sub"), None), P(), P(), P(), P(), P("sub", None, None)),
        check_vma=False,
    )
```

```python
import jax
import jax.numpy as jnp
from jax import lax
from jax.sharding import Mesh, PartitionSpec as P
import numpy as np

TB = 128
TPB = 8
SLOT = 8
NHUB = 2
DOM = ("dy", "dx", "dz")


HIGHEST_PREC = lax.Precision.HIGHEST


def one_hot_codes(code_rows, code_count, out_type):
    return (code_rows[..., None] == jnp.arange(code_count, dtype=jnp.int32)).astype(out_type)


def decode(code_rows, complete_codebooks):
    indicator_rows = one_hot_codes(code_rows, complete_codebooks.shape[1], jnp.bfloat16)
    rows = jnp.einsum(
        "feu,euq->feq", indicator_rows, complete_codebooks, preferred_element_type=jnp.float32
    )
    return rows.astype(jnp.bfloat16).reshape(code_rows.shape[0], -1)


def fold_books(code_rows, gradients, code_count):
    book_count = code_rows.shape[1]
    indicator_rows = one_hot_codes(code_rows, code_count, jnp.bfloat16)
    pieces = gradients.reshape(gradients.shape[0], book_count, -1)
    upper_bound = pieces.astype(jnp.bfloat16)
    lower_bound = (pieces - upper_bound.astype(jnp.float32)).astype(jnp.bfloat16)
    upper_half_sum = jnp.einsum(
        "fco,fcg->cog", indicator_rows, upper_bound, preferred_element_type=jnp.float32
    )
    lower_half_sum = jnp.einsum(
        "fco,fcg->cog", indicator_rows, lower_bound, preferred_element_type=jnp.float32
    )
    return upper_half_sum + lower_half_sum


def all_sum(grad_w_msg, grad_w_self, part_alpha, part_basis, book_grad, dom_axes):
    sub_index = lax.axis_index("sub")
    width = grad_w_msg.shape[1]
    share = book_grad.shape[0] // 2
    dense = [grad_w_msg, grad_w_self, part_basis, part_alpha.reshape(-1, width)]

    def half_of(h):
        pieces = [lax.dynamic_slice_in_dim(x, h * (x.shape[0] // 2), x.shape[0] // 2, 0) for x in dense]
        pieces.append(lax.dynamic_slice_in_dim(book_grad, h * share, share, 0).reshape(-1, width))
        return jnp.concatenate(pieces, axis=0)

    swap = [(0, 1), (1, 0)]
    mine = half_of(sub_index) + lax.ppermute(half_of(1 - sub_index), "sub", swap)
    rows = mine.shape[0]
    shapes = []
    piece = mine
    for stage, (axis, size) in enumerate(dom_axes):
        shapes.append(piece.shape)
        lanes = piece.shape[-1]
        if piece.shape[0] % size:
            lanes = 256
        chunks = piece.reshape(size, -1, lanes)
        if stage == 0:
            chunks = chunks.astype(jnp.bfloat16)
        received = lax.all_to_all(chunks, axis, 0, 0, tiled=True)
        piece = jnp.sum(received.astype(jnp.float32), axis=0)
    piece = piece.astype(jnp.bfloat16)
    for (axis, size), shape in reversed(list(zip(dom_axes, shapes))):
        spread = jnp.broadcast_to(piece[None], (size,) + piece.shape)
        piece = lax.all_to_all(spread, axis, 0, 0, tiled=True).reshape(shape)
    own_half = piece
    dense_rows = rows - share * book_grad.shape[1] * book_grad.shape[2] // width
    own_dense = own_half[:dense_rows]
    other_dense = lax.ppermute(own_dense, "sub", swap)
    low = jnp.where(sub_index == 0, own_dense, other_dense).astype(jnp.float32)
    high = jnp.where(sub_index == 0, other_dense, own_dense).astype(jnp.float32)
    out = []
    start = 0
    for x in dense:
        r = x.shape[0] // 2
        out.append(jnp.concatenate([low[start : start + r], high[start : start + r]], axis=0))
        start += r
    out[3] = out[3].reshape(part_alpha.shape)
    books_mine = own_half[dense_rows:].astype(jnp.float32).reshape((share,) + book_grad.shape[1:])
    return out + [books_mine]


def shards(
    dom_axes,
    codes,
    books,
    alpha,
    basis,
    w_msg,
    w_self,
    tiles,
    tile_src,
    tile_rel,
    send_rows,
    send_count,
    hub_owner,
    cotangent,
):
    rows_dev, book_count = codes.shape
    code_count = books.shape[1]
    model_width = w_msg.shape[0]
    tile_count = tiles.shape[0]
    block_count = tile_count // TPB
    complete_codebooks = lax.all_gather(books, "sub", axis=0, tiled=True)
    rel_table = jnp.dot(alpha, basis, precision=HIGHEST_PREC, preferred_element_type=jnp.float32)
    targets = send_rows[0, 0]
    part_count = targets.shape[0]
    slot_valid = jnp.arange(SLOT, dtype=jnp.int32)[None, :] < send_count[0, 0][:, None]
    out_codes = jnp.where(slot_valid[:, :, None], codes[targets], -1).reshape(part_count, -1)
    own_codes = jnp.broadcast_to(codes.reshape(1, -1), (part_count, codes.size))
    room = -(-(codes.size + out_codes.shape[1]) // 128) * 128
    filler = jnp.zeros((part_count, room - codes.size - out_codes.shape[1]), jnp.int32)
    payload = jnp.concatenate([own_codes, out_codes, filler], axis=1)
    incoming = lax.all_to_all(payload, DOM, 0, 0, tiled=True)
    recv_codes = incoming[:, codes.size : codes.size + out_codes.shape[1]].reshape(-1, book_count)
    hub_codes = [
        incoming[hub_owner[hub_index], : codes.size].reshape(codes.shape)
        for hub_index in range(NHUB)
    ]
    table_codes = jnp.concatenate([codes, recv_codes] + hub_codes, axis=0)
    local_rows = decode(codes, complete_codebooks)
    table = jnp.concatenate(
        [local_rows, decode(table_codes[rows_dev:], complete_codebooks)], axis=0
    )
    blocks = table.reshape(-1, TB, model_width)
    tile_blocks = tiles.reshape(block_count, TPB, TB, TB)
    picked = blocks[tile_src]
    scale = rel_table[tile_rel]
    composed = (picked.astype(jnp.float32) * scale[:, None, :]).astype(jnp.bfloat16)
    aggregate = jnp.einsum(
        "btij,btjd->bid",
        tile_blocks,
        composed.reshape(block_count, TPB, TB, model_width),
        preferred_element_type=jnp.float32,
    ).astype(jnp.bfloat16).reshape(rows_dev, model_width)
    pre_act = jnp.dot(aggregate, w_msg, preferred_element_type=jnp.float32) + jnp.dot(
        local_rows, w_self, preferred_element_type=jnp.float32
    )
    activated = jnp.tanh(pre_act)
    output = activated.astype(jnp.bfloat16)
    grad_pre = (cotangent.astype(jnp.float32) * (1.0 - activated * activated)).astype(jnp.bfloat16)
    contract_rows = (((0,), (0,)), ((), ()))
    contract_cols = (((1,), (1,)), ((), ()))
    grad_w_msg = lax.dot_general(
        aggregate, grad_pre, contract_rows, preferred_element_type=jnp.float32
    )
    grad_w_self = lax.dot_general(
        local_rows, grad_pre, contract_rows, preferred_element_type=jnp.float32
    )
    grad_agg = lax.dot_general(
        grad_pre, w_msg, contract_cols, preferred_element_type=jnp.float32
    ).astype(jnp.bfloat16)
    grad_self = lax.dot_general(grad_pre, w_self, contract_cols, preferred_element_type=jnp.float32)
    grad_blocks = grad_agg.reshape(block_count, TB, model_width)
    grad_comp = jnp.einsum(
        "btji,bjd->btid", tile_blocks, grad_blocks, preferred_element_type=jnp.float32
    ).reshape(tile_count, TB, model_width)
    rel_rows = jnp.sum(grad_comp * picked.astype(jnp.float32), axis=1)
    rel_grad = jnp.zeros(rel_table.shape, jnp.float32).at[tile_rel].add(rel_rows)
    tile_codes = table_codes.reshape(-1, TB, book_count)[tile_src].reshape(-1, book_count)
    contrib = (grad_comp * scale[:, None, :]).reshape(-1, model_width)
    book_grad = fold_books(tile_codes, contrib, code_count) + fold_books(codes, grad_self, code_count)
    part_alpha = jnp.dot(
        rel_grad, basis.T, precision=HIGHEST_PREC, preferred_element_type=jnp.float32
    )
    part_basis = jnp.dot(
        alpha.T, rel_grad, precision=HIGHEST_PREC, preferred_element_type=jnp.float32
    )
    total_msg, total_self, grad_basis, grad_alpha, grad_books = all_sum(
        grad_w_msg, grad_w_self, part_alpha, part_basis, book_grad, dom_axes
    )
    return (output, total_msg, total_self, grad_alpha, grad_basis, grad_books)


def split_mesh(mesh):
    grid = np.asarray(mesh.devices)
    try:
        coords = np.array([d.coords for d in grid.reshape(-1)]).reshape(grid.shape + (-1,))
    except (AttributeError, ValueError):
        return None
    ny, nx, nz = (len(np.unique(coords[..., k])) for k in (1, 0, 2))
    if ny * nx * nz != grid.shape[0]:
        return None
    cube = coords.reshape(ny, nx, nz, grid.shape[1], -1)
    for axis, k in ((0, 1), (1, 0), (2, 2)):
        others = [c for c in range(3) if c != k]
        if np.any(np.diff(cube[..., others], axis=axis) != 0):
            return None
    return Mesh(grid.reshape(ny, nx, nz, grid.shape[1]), DOM + ("sub",)), (ny, nx, nz)


def solution(mesh):
    found = split_mesh(mesh)
    assert found is not None
    fine_mesh, (ny, nx, nz) = found
    dom_axes = ((("dy", "dx"), ny * nx), ("dz", nz))

    def run(*args):
        return shards(dom_axes, *args)

    rows = P(DOM + ("sub",))
    return jax.shard_map(
        run,
        mesh=fine_mesh,
        in_specs=(
            P(DOM + ("sub",), None),
            P("sub", None, None),
            P(),
            P(),
            P(),
            P(),
            P(DOM + ("sub",), None, None),
            rows,
            rows,
            P(DOM, "sub", None, None),
            P(DOM, "sub", None),
            P(),
            P(DOM + ("sub",), None),
        ),
        out_specs=(P(DOM + ("sub",), None), P(), P(), P(), P(), P("sub", None, None)),
        check_vma=False,
    )
```

```python
import jax
import jax.numpy as jnp
from jax import lax
from jax.sharding import Mesh, PartitionSpec as P
import numpy as np

TB = 128
TPB = 8
SLOT = 8
NHUB = 2
DOM = ("dy", "dx", "dz")


HIGHEST_PREC = lax.Precision.HIGHEST


def one_hot_codes(code_rows, code_count, out_type):
    return (code_rows[..., None] == jnp.arange(code_count, dtype=jnp.int32)).astype(out_type)


def decode(code_rows, complete_codebooks):
    indicator_rows = one_hot_codes(code_rows, complete_codebooks.shape[1], jnp.bfloat16)
    rows = jnp.einsum(
        "feu,euq->feq", indicator_rows, complete_codebooks, preferred_element_type=jnp.float32
    )
    return rows.astype(jnp.bfloat16).reshape(code_rows.shape[0], -1)


def fold_books(code_rows, gradients, code_count):
    book_count = code_rows.shape[1]
    slice_width = gradients.shape[1] // book_count
    codes_hot = jnp.arange(code_count, dtype=jnp.int32)
    folded = []
    for book_index in range(book_count):
        piece = gradients[:, book_index * slice_width : (book_index + 1) * slice_width]
        upper_bound = piece.astype(jnp.bfloat16)
        lower_bound = (piece - upper_bound.astype(jnp.float32)).astype(jnp.bfloat16)
        both = jnp.concatenate([upper_bound, lower_bound], axis=1)
        indicator_rows = (code_rows[:, book_index][:, None] == codes_hot).astype(jnp.bfloat16)
        summed = lax.dot_general(
            indicator_rows, both, (((0,), (0,)), ((), ())), preferred_element_type=jnp.float32
        )
        folded.append(summed[:, :slice_width] + summed[:, slice_width:])
    return jnp.stack(folded)


def all_sum(grad_w_msg, grad_w_self, part_alpha, part_basis, book_grad, dom_axes):
    sub_index = lax.axis_index("sub")
    width = grad_w_msg.shape[1]
    share = book_grad.shape[0] // 2
    dense = [grad_w_msg, grad_w_self, part_basis, part_alpha.reshape(-1, width)]

    def half_of(h):
        pieces = [lax.dynamic_slice_in_dim(x, h * (x.shape[0] // 2), x.shape[0] // 2, 0) for x in dense]
        pieces.append(lax.dynamic_slice_in_dim(book_grad, h * share, share, 0).reshape(-1, width))
        return jnp.concatenate(pieces, axis=0)

    swap = [(0, 1), (1, 0)]
    mine = half_of(sub_index) + lax.ppermute(half_of(1 - sub_index), "sub", swap)
    rows = mine.shape[0]
    shapes = []
    piece = mine
    for stage, (axis, size) in enumerate(dom_axes):
        shapes.append(piece.shape)
        lanes = piece.shape[-1]
        if piece.shape[0] % size:
            lanes = 256
        chunks = piece.reshape(size, -1, lanes)
        if stage == 0:
            chunks = chunks.astype(jnp.bfloat16)
        received = lax.all_to_all(chunks, axis, 0, 0, tiled=True)
        piece = jnp.sum(received.astype(jnp.float32), axis=0)
    piece = piece.astype(jnp.bfloat16)
    for (axis, size), shape in reversed(list(zip(dom_axes, shapes))):
        spread = jnp.broadcast_to(piece[None], (size,) + piece.shape)
        piece = lax.all_to_all(spread, axis, 0, 0, tiled=True).reshape(shape)
    own_half = piece
    dense_rows = rows - share * book_grad.shape[1] * book_grad.shape[2] // width
    own_dense = own_half[:dense_rows]
    other_dense = lax.ppermute(own_dense, "sub", swap)
    low = jnp.where(sub_index == 0, own_dense, other_dense).astype(jnp.float32)
    high = jnp.where(sub_index == 0, other_dense, own_dense).astype(jnp.float32)
    out = []
    start = 0
    for x in dense:
        r = x.shape[0] // 2
        out.append(jnp.concatenate([low[start : start + r], high[start : start + r]], axis=0))
        start += r
    out[3] = out[3].reshape(part_alpha.shape)
    books_mine = own_half[dense_rows:].astype(jnp.float32).reshape((share,) + book_grad.shape[1:])
    return out + [books_mine]


def shards(
    dom_axes,
    codes,
    books,
    alpha,
    basis,
    w_msg,
    w_self,
    tiles,
    tile_src,
    tile_rel,
    send_rows,
    send_count,
    hub_owner,
    cotangent,
):
    rows_dev, book_count = codes.shape
    code_count = books.shape[1]
    model_width = w_msg.shape[0]
    tile_count = tiles.shape[0]
    block_count = tile_count // TPB
    complete_codebooks = lax.all_gather(books, "sub", axis=0, tiled=True)
    rel_table = jnp.dot(alpha, basis, precision=HIGHEST_PREC, preferred_element_type=jnp.float32)
    targets = send_rows[0, 0]
    part_count = targets.shape[0]
    slot_valid = jnp.arange(SLOT, dtype=jnp.int32)[None, :] < send_count[0, 0][:, None]
    out_codes = jnp.where(slot_valid[:, :, None], codes[targets], -1).reshape(part_count, -1)
    own_codes = jnp.broadcast_to(codes.reshape(1, -1), (part_count, codes.size))
    room = -(-(codes.size + out_codes.shape[1]) // 128) * 128
    filler = jnp.zeros((part_count, room - codes.size - out_codes.shape[1]), jnp.int32)
    payload = jnp.concatenate([own_codes, out_codes, filler], axis=1)
    incoming = lax.all_to_all(payload, DOM, 0, 0, tiled=True)
    recv_codes = incoming[:, codes.size : codes.size + out_codes.shape[1]].reshape(-1, book_count)
    hub_codes = [
        incoming[hub_owner[hub_index], : codes.size].reshape(codes.shape)
        for hub_index in range(NHUB)
    ]
    table_codes = jnp.concatenate([codes, recv_codes] + hub_codes, axis=0)
    local_rows = decode(codes, complete_codebooks)
    table = jnp.concatenate(
        [local_rows, decode(table_codes[rows_dev:], complete_codebooks)], axis=0
    )
    blocks = table.reshape(-1, TB, model_width)
    tile_blocks = tiles.reshape(block_count, TPB, TB, TB)
    picked = blocks[tile_src]
    scale = rel_table[tile_rel]
    composed = (picked.astype(jnp.float32) * scale[:, None, :]).astype(jnp.bfloat16)
    aggregate = jnp.einsum(
        "btij,btjd->bid",
        tile_blocks,
        composed.reshape(block_count, TPB, TB, model_width),
        preferred_element_type=jnp.float32,
    ).astype(jnp.bfloat16).reshape(rows_dev, model_width)
    pre_act = jnp.dot(aggregate, w_msg, preferred_element_type=jnp.float32) + jnp.dot(
        local_rows, w_self, preferred_element_type=jnp.float32
    )
    activated = jnp.tanh(pre_act)
    output = activated.astype(jnp.bfloat16)
    grad_pre = (cotangent.astype(jnp.float32) * (1.0 - activated * activated)).astype(jnp.bfloat16)
    contract_rows = (((0,), (0,)), ((), ()))
    contract_cols = (((1,), (1,)), ((), ()))
    grad_w_msg = lax.dot_general(
        aggregate, grad_pre, contract_rows, preferred_element_type=jnp.float32
    )
    grad_w_self = lax.dot_general(
        local_rows, grad_pre, contract_rows, preferred_element_type=jnp.float32
    )
    grad_agg = lax.dot_general(
        grad_pre, w_msg, contract_cols, preferred_element_type=jnp.float32
    ).astype(jnp.bfloat16)
    grad_self = lax.dot_general(grad_pre, w_self, contract_cols, preferred_element_type=jnp.float32)
    grad_blocks = grad_agg.reshape(block_count, TB, model_width)
    grad_comp = jnp.einsum(
        "btji,bjd->btid", tile_blocks, grad_blocks, preferred_element_type=jnp.float32
    ).reshape(tile_count, TB, model_width)
    rel_rows = jnp.sum(grad_comp * picked.astype(jnp.float32), axis=1)
    rel_grad = jnp.zeros(rel_table.shape, jnp.float32).at[tile_rel].add(rel_rows)
    tile_codes = table_codes.reshape(-1, TB, book_count)[tile_src].reshape(-1, book_count)
    contrib = (grad_comp * scale[:, None, :]).reshape(-1, model_width)
    book_grad = fold_books(tile_codes, contrib, code_count) + fold_books(codes, grad_self, code_count)
    part_alpha = jnp.dot(
        rel_grad, basis.T, precision=HIGHEST_PREC, preferred_element_type=jnp.float32
    )
    part_basis = jnp.dot(
        alpha.T, rel_grad, precision=HIGHEST_PREC, preferred_element_type=jnp.float32
    )
    total_msg, total_self, grad_basis, grad_alpha, grad_books = all_sum(
        grad_w_msg, grad_w_self, part_alpha, part_basis, book_grad, dom_axes
    )
    return (output, total_msg, total_self, grad_alpha, grad_basis, grad_books)


def split_mesh(mesh):
    grid = np.asarray(mesh.devices)
    try:
        coords = np.array([d.coords for d in grid.reshape(-1)]).reshape(grid.shape + (-1,))
    except (AttributeError, ValueError):
        return None
    ny, nx, nz = (len(np.unique(coords[..., k])) for k in (1, 0, 2))
    if ny * nx * nz != grid.shape[0]:
        return None
    cube = coords.reshape(ny, nx, nz, grid.shape[1], -1)
    for axis, k in ((0, 1), (1, 0), (2, 2)):
        others = [c for c in range(3) if c != k]
        if np.any(np.diff(cube[..., others], axis=axis) != 0):
            return None
    return Mesh(grid.reshape(ny, nx, nz, grid.shape[1]), DOM + ("sub",)), (ny, nx, nz)


def solution(mesh):
    found = split_mesh(mesh)
    assert found is not None
    fine_mesh, (ny, nx, nz) = found
    dom_axes = ((("dy", "dx"), ny * nx), ("dz", nz))

    def run(*args):
        return shards(dom_axes, *args)

    rows = P(DOM + ("sub",))
    return jax.shard_map(
        run,
        mesh=fine_mesh,
        in_specs=(
            P(DOM + ("sub",), None),
            P("sub", None, None),
            P(),
            P(),
            P(),
            P(),
            P(DOM + ("sub",), None, None),
            rows,
            rows,
            P(DOM, "sub", None, None),
            P(DOM, "sub", None),
            P(),
            P(DOM + ("sub",), None),
        ),
        out_specs=(P(DOM + ("sub",), None), P(), P(), P(), P(), P("sub", None, None)),
        check_vma=False,
    )
```

```python
import jax
import jax.numpy as jnp
from jax import lax
from jax.sharding import Mesh, PartitionSpec as P
import numpy as np

TB = 128
TPB = 8
SLOT = 8
NHUB = 2
DOM = ("dy", "dx", "dz")


HIGHEST_PREC = lax.Precision.HIGHEST


def one_hot_codes(code_rows, code_count, out_type):
    return (code_rows[..., None] == jnp.arange(code_count, dtype=jnp.int32)).astype(out_type)


def decode(code_rows, complete_codebooks):
    indicator_rows = one_hot_codes(code_rows, complete_codebooks.shape[1], jnp.bfloat16)
    rows = jnp.einsum(
        "feu,euq->feq", indicator_rows, complete_codebooks, preferred_element_type=jnp.float32
    )
    return rows.astype(jnp.bfloat16).reshape(code_rows.shape[0], -1)


def fold_books(code_rows, gradients, code_count):
    book_count = code_rows.shape[1]
    slice_width = gradients.shape[1] // book_count
    codes_hot = jnp.arange(code_count, dtype=jnp.int32)
    folded = []
    for book_index in range(book_count):
        piece = gradients[:, book_index * slice_width : (book_index + 1) * slice_width]
        upper_bound = piece.astype(jnp.bfloat16)
        lower_bound = (piece - upper_bound.astype(jnp.float32)).astype(jnp.bfloat16)
        both = jnp.concatenate([upper_bound, lower_bound], axis=1)
        indicator_rows = (code_rows[:, book_index][:, None] == codes_hot).astype(jnp.bfloat16)
        summed = lax.dot_general(
            indicator_rows, both, (((0,), (0,)), ((), ())), preferred_element_type=jnp.float32
        )
        folded.append(summed[:, :slice_width] + summed[:, slice_width:])
    return jnp.stack(folded)


def all_sum(grad_w_msg, grad_w_self, part_alpha, part_basis, book_grad, dom_axes):
    sub_index = lax.axis_index("sub")
    width = grad_w_msg.shape[1]
    share = book_grad.shape[0] // 2
    dense = [grad_w_msg, grad_w_self, part_basis, part_alpha.reshape(-1, width)]

    def half_of(h):
        pieces = [lax.dynamic_slice_in_dim(x, h * (x.shape[0] // 2), x.shape[0] // 2, 0) for x in dense]
        pieces.append(lax.dynamic_slice_in_dim(book_grad, h * share, share, 0).reshape(-1, width))
        return jnp.concatenate(pieces, axis=0)

    swap = [(0, 1), (1, 0)]
    mine = half_of(sub_index) + lax.ppermute(half_of(1 - sub_index), "sub", swap)
    rows = mine.shape[0]
    shapes = []
    piece = mine
    for stage, (axis, size) in enumerate(dom_axes):
        shapes.append(piece.shape)
        lanes = piece.shape[-1]
        if piece.shape[0] % size:
            lanes = 256
        chunks = piece.reshape(size, -1, lanes)
        if stage == 0:
            chunks = chunks.astype(jnp.bfloat16)
        received = lax.all_to_all(chunks, axis, 0, 0, tiled=True)
        piece = jnp.sum(received.astype(jnp.float32), axis=0)
    piece = piece.astype(jnp.bfloat16)
    for (axis, size), shape in reversed(list(zip(dom_axes, shapes))):
        piece = lax.all_gather(piece, axis, axis=0, tiled=True).reshape(shape)
    own_half = piece
    dense_rows = rows - share * book_grad.shape[1] * book_grad.shape[2] // width
    own_dense = own_half[:dense_rows]
    other_dense = lax.ppermute(own_dense, "sub", swap)
    low = jnp.where(sub_index == 0, own_dense, other_dense).astype(jnp.float32)
    high = jnp.where(sub_index == 0, other_dense, own_dense).astype(jnp.float32)
    out = []
    start = 0
    for x in dense:
        r = x.shape[0] // 2
        out.append(jnp.concatenate([low[start : start + r], high[start : start + r]], axis=0))
        start += r
    out[3] = out[3].reshape(part_alpha.shape)
    books_mine = own_half[dense_rows:].astype(jnp.float32).reshape((share,) + book_grad.shape[1:])
    return out + [books_mine]


def shards(
    dom_axes,
    codes,
    books,
    alpha,
    basis,
    w_msg,
    w_self,
    tiles,
    tile_src,
    tile_rel,
    send_rows,
    send_count,
    hub_owner,
    cotangent,
):
    rows_dev, book_count = codes.shape
    code_count = books.shape[1]
    model_width = w_msg.shape[0]
    tile_count = tiles.shape[0]
    block_count = tile_count // TPB
    complete_codebooks = lax.all_gather(books, "sub", axis=0, tiled=True)
    rel_table = jnp.dot(alpha, basis, precision=HIGHEST_PREC, preferred_element_type=jnp.float32)
    targets = send_rows[0, 0]
    part_count = targets.shape[0]
    slot_valid = jnp.arange(SLOT, dtype=jnp.int32)[None, :] < send_count[0, 0][:, None]
    out_codes = jnp.where(slot_valid[:, :, None], codes[targets], -1).reshape(part_count, -1)
    own_codes = jnp.broadcast_to(codes.reshape(1, -1), (part_count, codes.size))
    room = -(-(codes.size + out_codes.shape[1]) // 128) * 128
    filler = jnp.zeros((part_count, room - codes.size - out_codes.shape[1]), jnp.int32)
    payload = jnp.concatenate([own_codes, out_codes, filler], axis=1)
    incoming = lax.all_to_all(payload, DOM, 0, 0, tiled=True)
    recv_codes = incoming[:, codes.size : codes.size + out_codes.shape[1]].reshape(-1, book_count)
    hub_codes = [
        incoming[hub_owner[hub_index], : codes.size].reshape(codes.shape)
        for hub_index in range(NHUB)
    ]
    table_codes = jnp.concatenate([codes, recv_codes] + hub_codes, axis=0)
    local_rows = decode(codes, complete_codebooks)
    table = jnp.concatenate(
        [local_rows, decode(table_codes[rows_dev:], complete_codebooks)], axis=0
    )
    blocks = table.reshape(-1, TB, model_width)
    tile_blocks = tiles.reshape(block_count, TPB, TB, TB)
    picked = blocks[tile_src]
    scale = rel_table[tile_rel]
    composed = (picked.astype(jnp.float32) * scale[:, None, :]).astype(jnp.bfloat16)
    aggregate = jnp.einsum(
        "btij,btjd->bid",
        tile_blocks,
        composed.reshape(block_count, TPB, TB, model_width),
        preferred_element_type=jnp.float32,
    ).astype(jnp.bfloat16).reshape(rows_dev, model_width)
    pre_act = jnp.dot(aggregate, w_msg, preferred_element_type=jnp.float32) + jnp.dot(
        local_rows, w_self, preferred_element_type=jnp.float32
    )
    activated = jnp.tanh(pre_act)
    output = activated.astype(jnp.bfloat16)
    grad_pre = (cotangent.astype(jnp.float32) * (1.0 - activated * activated)).astype(jnp.bfloat16)
    contract_rows = (((0,), (0,)), ((), ()))
    contract_cols = (((1,), (1,)), ((), ()))
    grad_w_msg = lax.dot_general(
        aggregate, grad_pre, contract_rows, preferred_element_type=jnp.float32
    )
    grad_w_self = lax.dot_general(
        local_rows, grad_pre, contract_rows, preferred_element_type=jnp.float32
    )
    grad_agg = lax.dot_general(
        grad_pre, w_msg, contract_cols, preferred_element_type=jnp.float32
    ).astype(jnp.bfloat16)
    grad_self = lax.dot_general(grad_pre, w_self, contract_cols, preferred_element_type=jnp.float32)
    grad_blocks = grad_agg.reshape(block_count, TB, model_width)
    grad_comp = jnp.einsum(
        "btji,bjd->btid", tile_blocks, grad_blocks, preferred_element_type=jnp.float32
    ).reshape(tile_count, TB, model_width)
    rel_rows = jnp.sum(grad_comp * picked.astype(jnp.float32), axis=1)
    rel_grad = jnp.zeros(rel_table.shape, jnp.float32).at[tile_rel].add(rel_rows)
    tile_codes = table_codes.reshape(-1, TB, book_count)[tile_src].reshape(-1, book_count)
    contrib = (grad_comp * scale[:, None, :]).reshape(-1, model_width)
    book_grad = fold_books(tile_codes, contrib, code_count) + fold_books(codes, grad_self, code_count)
    part_alpha = jnp.dot(
        rel_grad, basis.T, precision=HIGHEST_PREC, preferred_element_type=jnp.float32
    )
    part_basis = jnp.dot(
        alpha.T, rel_grad, precision=HIGHEST_PREC, preferred_element_type=jnp.float32
    )
    total_msg, total_self, grad_basis, grad_alpha, grad_books = all_sum(
        grad_w_msg, grad_w_self, part_alpha, part_basis, book_grad, dom_axes
    )
    return (output, total_msg, total_self, grad_alpha, grad_basis, grad_books)


def split_mesh(mesh):
    grid = np.asarray(mesh.devices)
    try:
        coords = np.array([d.coords for d in grid.reshape(-1)]).reshape(grid.shape + (-1,))
    except (AttributeError, ValueError):
        return None
    ny, nx, nz = (len(np.unique(coords[..., k])) for k in (1, 0, 2))
    if ny * nx * nz != grid.shape[0]:
        return None
    cube = coords.reshape(ny, nx, nz, grid.shape[1], -1)
    for axis, k in ((0, 1), (1, 0), (2, 2)):
        others = [c for c in range(3) if c != k]
        if np.any(np.diff(cube[..., others], axis=axis) != 0):
            return None
    return Mesh(grid.reshape(ny, nx, nz, grid.shape[1]), DOM + ("sub",)), (ny, nx, nz)


def solution(mesh):
    found = split_mesh(mesh)
    assert found is not None
    fine_mesh, (ny, nx, nz) = found
    dom_axes = ((("dy", "dx"), ny * nx), ("dz", nz))

    def run(*args):
        return shards(dom_axes, *args)

    rows = P(DOM + ("sub",))
    return jax.shard_map(
        run,
        mesh=fine_mesh,
        in_specs=(
            P(DOM + ("sub",), None),
            P("sub", None, None),
            P(),
            P(),
            P(),
            P(),
            P(DOM + ("sub",), None, None),
            rows,
            rows,
            P(DOM, "sub", None, None),
            P(DOM, "sub", None),
            P(),
            P(DOM + ("sub",), None),
        ),
        out_specs=(P(DOM + ("sub",), None), P(), P(), P(), P(), P("sub", None, None)),
        check_vma=False,
    )
```

```python
import jax
import jax.numpy as jnp
from jax import lax
from jax.sharding import Mesh, PartitionSpec as P
import numpy as np

TB = 128
TPB = 8
SLOT = 8
NHUB = 2
DOM = ("dy", "dx", "dz")


HIGHEST_PREC = lax.Precision.HIGHEST


def one_hot_codes(code_rows, code_count, out_type):
    return (code_rows[..., None] == jnp.arange(code_count, dtype=jnp.int32)).astype(out_type)


def decode(code_rows, complete_codebooks):
    indicator_rows = one_hot_codes(code_rows, complete_codebooks.shape[1], jnp.bfloat16)
    rows = jnp.einsum(
        "feu,euq->feq", indicator_rows, complete_codebooks, preferred_element_type=jnp.float32
    )
    return rows.astype(jnp.bfloat16).reshape(code_rows.shape[0], -1)


def fold_books(code_rows, gradients, code_count):
    book_count = code_rows.shape[1]
    slice_width = gradients.shape[1] // book_count
    codes_hot = jnp.arange(code_count, dtype=jnp.int32)
    folded = []
    for book_index in range(book_count):
        piece = gradients[:, book_index * slice_width : (book_index + 1) * slice_width]
        upper_bound = piece.astype(jnp.bfloat16)
        lower_bound = (piece - upper_bound.astype(jnp.float32)).astype(jnp.bfloat16)
        both = jnp.concatenate([upper_bound, lower_bound], axis=1)
        indicator_rows = (code_rows[:, book_index][:, None] == codes_hot).astype(jnp.bfloat16)
        summed = lax.dot_general(
            indicator_rows, both, (((0,), (0,)), ((), ())), preferred_element_type=jnp.float32
        )
        folded.append(summed[:, :slice_width] + summed[:, slice_width:])
    return jnp.stack(folded)


def all_sum(grad_w_msg, grad_w_self, part_alpha, part_basis, book_grad, dom_axes):
    sub_index = lax.axis_index("sub")
    width = grad_w_msg.shape[1]
    share = book_grad.shape[0] // 2
    dense = [grad_w_msg, grad_w_self, part_basis, part_alpha.reshape(-1, width)]

    def half_of(h):
        pieces = [lax.dynamic_slice_in_dim(x, h * (x.shape[0] // 2), x.shape[0] // 2, 0) for x in dense]
        pieces.append(lax.dynamic_slice_in_dim(book_grad, h * share, share, 0).reshape(-1, width))
        return jnp.concatenate(pieces, axis=0)

    swap = [(0, 1), (1, 0)]
    mine = half_of(sub_index) + lax.ppermute(half_of(1 - sub_index), "sub", swap)
    rows = mine.shape[0]
    shapes = []
    piece = mine
    for stage, (axis, size) in enumerate(dom_axes):
        shapes.append(piece.shape)
        lanes = piece.shape[-1]
        if piece.shape[0] % size:
            lanes = 256
        chunks = piece.reshape(size, -1, lanes)
        if stage == 0:
            chunks = chunks.astype(jnp.bfloat16)
        received = lax.all_to_all(chunks, axis, 0, 0, tiled=True)
        piece = jnp.sum(received.astype(jnp.float32), axis=0)
    piece = piece.astype(jnp.bfloat16)
    for (axis, size), shape in reversed(list(zip(dom_axes, shapes))):
        spread = jnp.broadcast_to(piece[None], (size,) + piece.shape)
        piece = lax.all_to_all(spread, axis, 0, 0, tiled=True).reshape(shape)
    own_half = piece
    dense_rows = rows - share * book_grad.shape[1] * book_grad.shape[2] // width
    own_dense = own_half[:dense_rows]
    other_dense = lax.ppermute(own_dense, "sub", swap)
    low = jnp.where(sub_index == 0, own_dense, other_dense).astype(jnp.float32)
    high = jnp.where(sub_index == 0, other_dense, own_dense).astype(jnp.float32)
    out = []
    start = 0
    for x in dense:
        r = x.shape[0] // 2
        out.append(jnp.concatenate([low[start : start + r], high[start : start + r]], axis=0))
        start += r
    out[3] = out[3].reshape(part_alpha.shape)
    books_mine = own_half[dense_rows:].astype(jnp.float32).reshape((share,) + book_grad.shape[1:])
    return out + [books_mine]


def shards(
    dom_axes,
    codes,
    books,
    alpha,
    basis,
    w_msg,
    w_self,
    tiles,
    tile_src,
    tile_rel,
    send_rows,
    send_count,
    hub_owner,
    cotangent,
):
    rows_dev, book_count = codes.shape
    code_count = books.shape[1]
    model_width = w_msg.shape[0]
    tile_count = tiles.shape[0]
    block_count = tile_count // TPB
    complete_codebooks = lax.all_gather(books, "sub", axis=0, tiled=True)
    rel_table = jnp.dot(alpha, basis, precision=HIGHEST_PREC, preferred_element_type=jnp.float32)
    targets = send_rows[0, 0]
    part_count = targets.shape[0]
    slot_valid = jnp.arange(SLOT, dtype=jnp.int32)[None, :] < send_count[0, 0][:, None]
    target_hot = one_hot_codes(targets.reshape(-1), rows_dev, jnp.bfloat16)
    picked_codes = jnp.dot(
        target_hot, codes.astype(jnp.bfloat16), preferred_element_type=jnp.float32
    ).astype(jnp.int32).reshape(targets.shape + (book_count,))
    out_codes = jnp.where(slot_valid[:, :, None], picked_codes, -1).reshape(part_count, -1)
    own_codes = jnp.broadcast_to(codes.reshape(1, -1), (part_count, codes.size))
    room = -(-(codes.size + out_codes.shape[1]) // 128) * 128
    filler = jnp.zeros((part_count, room - codes.size - out_codes.shape[1]), jnp.int32)
    payload = jnp.concatenate([own_codes, out_codes, filler], axis=1)
    incoming = lax.all_to_all(payload, DOM, 0, 0, tiled=True)
    recv_codes = incoming[:, codes.size : codes.size + out_codes.shape[1]].reshape(-1, book_count)
    hub_codes = [
        incoming[hub_owner[hub_index], : codes.size].reshape(codes.shape)
        for hub_index in range(NHUB)
    ]
    table_codes = jnp.concatenate([codes, recv_codes] + hub_codes, axis=0)
    local_rows = decode(codes, complete_codebooks)
    table = jnp.concatenate(
        [local_rows, decode(table_codes[rows_dev:], complete_codebooks)], axis=0
    )
    blocks = table.reshape(-1, TB, model_width)
    tile_blocks = tiles.reshape(block_count, TPB, TB, TB)
    picked = blocks[tile_src]
    scale = rel_table[tile_rel]
    composed = (picked.astype(jnp.float32) * scale[:, None, :]).astype(jnp.bfloat16)
    aggregate = jnp.einsum(
        "btij,btjd->bid",
        tile_blocks,
        composed.reshape(block_count, TPB, TB, model_width),
        preferred_element_type=jnp.float32,
    ).astype(jnp.bfloat16).reshape(rows_dev, model_width)
    pre_act = jnp.dot(aggregate, w_msg, preferred_element_type=jnp.float32) + jnp.dot(
        local_rows, w_self, preferred_element_type=jnp.float32
    )
    activated = jnp.tanh(pre_act)
    output = activated.astype(jnp.bfloat16)
    grad_pre = (cotangent.astype(jnp.float32) * (1.0 - activated * activated)).astype(jnp.bfloat16)
    contract_rows = (((0,), (0,)), ((), ()))
    contract_cols = (((1,), (1,)), ((), ()))
    grad_w_msg = lax.dot_general(
        aggregate, grad_pre, contract_rows, preferred_element_type=jnp.float32
    )
    grad_w_self = lax.dot_general(
        local_rows, grad_pre, contract_rows, preferred_element_type=jnp.float32
    )
    grad_agg = lax.dot_general(
        grad_pre, w_msg, contract_cols, preferred_element_type=jnp.float32
    ).astype(jnp.bfloat16)
    grad_self = lax.dot_general(grad_pre, w_self, contract_cols, preferred_element_type=jnp.float32)
    grad_blocks = grad_agg.reshape(block_count, TB, model_width)
    grad_comp = jnp.einsum(
        "btji,bjd->btid", tile_blocks, grad_blocks, preferred_element_type=jnp.float32
    ).reshape(tile_count, TB, model_width)
    rel_rows = jnp.sum(grad_comp * picked.astype(jnp.float32), axis=1)
    rel_grad = jnp.zeros(rel_table.shape, jnp.float32).at[tile_rel].add(rel_rows)
    tile_codes = table_codes.reshape(-1, TB, book_count)[tile_src].reshape(-1, book_count)
    contrib = (grad_comp * scale[:, None, :]).reshape(-1, model_width)
    book_grad = fold_books(tile_codes, contrib, code_count) + fold_books(codes, grad_self, code_count)
    part_alpha = jnp.dot(
        rel_grad, basis.T, precision=HIGHEST_PREC, preferred_element_type=jnp.float32
    )
    part_basis = jnp.dot(
        alpha.T, rel_grad, precision=HIGHEST_PREC, preferred_element_type=jnp.float32
    )
    total_msg, total_self, grad_basis, grad_alpha, grad_books = all_sum(
        grad_w_msg, grad_w_self, part_alpha, part_basis, book_grad, dom_axes
    )
    return (output, total_msg, total_self, grad_alpha, grad_basis, grad_books)


def split_mesh(mesh):
    grid = np.asarray(mesh.devices)
    try:
        coords = np.array([d.coords for d in grid.reshape(-1)]).reshape(grid.shape + (-1,))
    except (AttributeError, ValueError):
        return None
    ny, nx, nz = (len(np.unique(coords[..., k])) for k in (1, 0, 2))
    if ny * nx * nz != grid.shape[0]:
        return None
    cube = coords.reshape(ny, nx, nz, grid.shape[1], -1)
    for axis, k in ((0, 1), (1, 0), (2, 2)):
        others = [c for c in range(3) if c != k]
        if np.any(np.diff(cube[..., others], axis=axis) != 0):
            return None
    return Mesh(grid.reshape(ny, nx, nz, grid.shape[1]), DOM + ("sub",)), (ny, nx, nz)


def solution(mesh):
    found = split_mesh(mesh)
    assert found is not None
    fine_mesh, (ny, nx, nz) = found
    dom_axes = ((("dy", "dx"), ny * nx), ("dz", nz))

    def run(*args):
        return shards(dom_axes, *args)

    rows = P(DOM + ("sub",))
    return jax.shard_map(
        run,
        mesh=fine_mesh,
        in_specs=(
            P(DOM + ("sub",), None),
            P("sub", None, None),
            P(),
            P(),
            P(),
            P(),
            P(DOM + ("sub",), None, None),
            rows,
            rows,
            P(DOM, "sub", None, None),
            P(DOM, "sub", None),
            P(),
            P(DOM + ("sub",), None),
        ),
        out_specs=(P(DOM + ("sub",), None), P(), P(), P(), P(), P("sub", None, None)),
        check_vma=False,
    )
```

```python
import jax
import jax.numpy as jnp
from jax import lax
from jax.sharding import Mesh, PartitionSpec as P
import numpy as np

TB = 128
TPB = 8
SLOT = 8
NHUB = 2
DOM = ("dy", "dx", "dz")


HIGHEST_PREC = lax.Precision.HIGHEST


def one_hot_codes(code_rows, code_count, out_type):
    return (code_rows[..., None] == jnp.arange(code_count, dtype=jnp.int32)).astype(out_type)


def decode(code_rows, complete_codebooks):
    indicator_rows = one_hot_codes(code_rows, complete_codebooks.shape[1], jnp.bfloat16)
    rows = jnp.einsum(
        "feu,euq->feq", indicator_rows, complete_codebooks, preferred_element_type=jnp.float32
    )
    return rows.astype(jnp.bfloat16).reshape(code_rows.shape[0], -1)


def fold_books(code_rows, gradients, code_count):
    book_count = code_rows.shape[1]
    slice_width = gradients.shape[1] // book_count
    codes_hot = jnp.arange(code_count, dtype=jnp.int32)
    folded = []
    for book_index in range(book_count):
        piece = gradients[:, book_index * slice_width : (book_index + 1) * slice_width]
        upper_bound = piece.astype(jnp.bfloat16)
        lower_bound = (piece - upper_bound.astype(jnp.float32)).astype(jnp.bfloat16)
        both = jnp.concatenate([upper_bound, lower_bound], axis=1)
        indicator_rows = (code_rows[:, book_index][:, None] == codes_hot).astype(jnp.bfloat16)
        summed = lax.dot_general(
            indicator_rows, both, (((0,), (0,)), ((), ())), preferred_element_type=jnp.float32
        )
        folded.append(summed[:, :slice_width] + summed[:, slice_width:])
    return jnp.stack(folded)


def all_sum(grad_w_msg, grad_w_self, part_alpha, part_basis, book_grad, dom_axes):
    sub_index = lax.axis_index("sub")
    width = grad_w_msg.shape[1]
    share = book_grad.shape[0] // 2
    dense = [grad_w_msg, grad_w_self, part_basis, part_alpha.reshape(-1, width)]

    lows = [x[: x.shape[0] // 2] for x in dense] + [book_grad[:share].reshape(-1, width)]
    highs = [x[x.shape[0] // 2 :] for x in dense] + [book_grad[share:].reshape(-1, width)]
    stacked = jnp.stack([jnp.concatenate(lows, axis=0), jnp.concatenate(highs, axis=0)])
    keep = lax.dynamic_index_in_dim(stacked, sub_index, 0, keepdims=False)
    give = lax.dynamic_index_in_dim(stacked, 1 - sub_index, 0, keepdims=False)
    swap = [(0, 1), (1, 0)]
    mine = keep + lax.ppermute(give, "sub", swap)
    rows = mine.shape[0]
    shapes = []
    piece = mine
    for stage, (axis, size) in enumerate(dom_axes):
        shapes.append(piece.shape)
        lanes = piece.shape[-1]
        if piece.shape[0] % size:
            lanes = 256
        chunks = piece.reshape(size, -1, lanes)
        if stage == 0:
            chunks = chunks.astype(jnp.bfloat16)
        received = lax.all_to_all(chunks, axis, 0, 0, tiled=True)
        piece = jnp.sum(received.astype(jnp.float32), axis=0)
    piece = piece.astype(jnp.bfloat16)
    for (axis, size), shape in reversed(list(zip(dom_axes, shapes))):
        spread = jnp.broadcast_to(piece[None], (size,) + piece.shape)
        piece = lax.all_to_all(spread, axis, 0, 0, tiled=True).reshape(shape)
    own_half = piece
    dense_rows = rows - share * book_grad.shape[1] * book_grad.shape[2] // width
    own_dense = own_half[:dense_rows]
    other_dense = lax.ppermute(own_dense, "sub", swap)
    low = jnp.where(sub_index == 0, own_dense, other_dense).astype(jnp.float32)
    high = jnp.where(sub_index == 0, other_dense, own_dense).astype(jnp.float32)
    out = []
    start = 0
    for x in dense:
        r = x.shape[0] // 2
        out.append(jnp.concatenate([low[start : start + r], high[start : start + r]], axis=0))
        start += r
    out[3] = out[3].reshape(part_alpha.shape)
    books_mine = own_half[dense_rows:].astype(jnp.float32).reshape((share,) + book_grad.shape[1:])
    return out + [books_mine]


def shards(
    dom_axes,
    codes,
    books,
    alpha,
    basis,
    w_msg,
    w_self,
    tiles,
    tile_src,
    tile_rel,
    send_rows,
    send_count,
    hub_owner,
    cotangent,
):
    rows_dev, book_count = codes.shape
    code_count = books.shape[1]
    model_width = w_msg.shape[0]
    tile_count = tiles.shape[0]
    block_count = tile_count // TPB
    complete_codebooks = lax.all_gather(books, "sub", axis=0, tiled=True)
    rel_table = jnp.dot(alpha, basis, precision=HIGHEST_PREC, preferred_element_type=jnp.float32)
    targets = send_rows[0, 0]
    part_count = targets.shape[0]
    slot_valid = jnp.arange(SLOT, dtype=jnp.int32)[None, :] < send_count[0, 0][:, None]
    target_hot = one_hot_codes(targets.reshape(-1), rows_dev, jnp.bfloat16)
    picked_codes = jnp.dot(
        target_hot, codes.astype(jnp.bfloat16), preferred_element_type=jnp.float32
    ).astype(jnp.int32).reshape(targets.shape + (book_count,))
    out_codes = jnp.where(slot_valid[:, :, None], picked_codes, -1).reshape(part_count, -1)
    own_codes = jnp.broadcast_to(codes.reshape(1, -1), (part_count, codes.size))
    room = -(-(codes.size + out_codes.shape[1]) // 128) * 128
    filler = jnp.zeros((part_count, room - codes.size - out_codes.shape[1]), jnp.int32)
    payload = jnp.concatenate([own_codes, out_codes, filler], axis=1)
    incoming = lax.all_to_all(payload, DOM, 0, 0, tiled=True)
    recv_codes = incoming[:, codes.size : codes.size + out_codes.shape[1]].reshape(-1, book_count)
    hub_codes = [
        incoming[hub_owner[hub_index], : codes.size].reshape(codes.shape)
        for hub_index in range(NHUB)
    ]
    table_codes = jnp.concatenate([codes, recv_codes] + hub_codes, axis=0)
    local_rows = decode(codes, complete_codebooks)
    table = jnp.concatenate(
        [local_rows, decode(table_codes[rows_dev:], complete_codebooks)], axis=0
    )
    blocks = table.reshape(-1, TB, model_width)
    tile_blocks = tiles.reshape(block_count, TPB, TB, TB)
    picked = blocks[tile_src]
    scale = rel_table[tile_rel]
    composed = (picked.astype(jnp.float32) * scale[:, None, :]).astype(jnp.bfloat16)
    aggregate = jnp.einsum(
        "btij,btjd->bid",
        tile_blocks,
        composed.reshape(block_count, TPB, TB, model_width),
        preferred_element_type=jnp.float32,
    ).astype(jnp.bfloat16).reshape(rows_dev, model_width)
    pre_act = jnp.dot(aggregate, w_msg, preferred_element_type=jnp.float32) + jnp.dot(
        local_rows, w_self, preferred_element_type=jnp.float32
    )
    activated = jnp.tanh(pre_act)
    output = activated.astype(jnp.bfloat16)
    grad_pre = (cotangent.astype(jnp.float32) * (1.0 - activated * activated)).astype(jnp.bfloat16)
    contract_rows = (((0,), (0,)), ((), ()))
    contract_cols = (((1,), (1,)), ((), ()))
    grad_w_msg = lax.dot_general(
        aggregate, grad_pre, contract_rows, preferred_element_type=jnp.float32
    )
    grad_w_self = lax.dot_general(
        local_rows, grad_pre, contract_rows, preferred_element_type=jnp.float32
    )
    grad_agg = lax.dot_general(
        grad_pre, w_msg, contract_cols, preferred_element_type=jnp.float32
    ).astype(jnp.bfloat16)
    grad_self = lax.dot_general(grad_pre, w_self, contract_cols, preferred_element_type=jnp.float32)
    grad_blocks = grad_agg.reshape(block_count, TB, model_width)
    grad_comp = jnp.einsum(
        "btji,bjd->btid", tile_blocks, grad_blocks, preferred_element_type=jnp.float32
    ).reshape(tile_count, TB, model_width)
    rel_rows = jnp.sum(grad_comp * picked.astype(jnp.float32), axis=1)
    rel_grad = jnp.zeros(rel_table.shape, jnp.float32).at[tile_rel].add(rel_rows)
    tile_codes = table_codes.reshape(-1, TB, book_count)[tile_src].reshape(-1, book_count)
    contrib = (grad_comp * scale[:, None, :]).reshape(-1, model_width)
    book_grad = fold_books(tile_codes, contrib, code_count) + fold_books(codes, grad_self, code_count)
    part_alpha = jnp.dot(
        rel_grad, basis.T, precision=HIGHEST_PREC, preferred_element_type=jnp.float32
    )
    part_basis = jnp.dot(
        alpha.T, rel_grad, precision=HIGHEST_PREC, preferred_element_type=jnp.float32
    )
    total_msg, total_self, grad_basis, grad_alpha, grad_books = all_sum(
        grad_w_msg, grad_w_self, part_alpha, part_basis, book_grad, dom_axes
    )
    return (output, total_msg, total_self, grad_alpha, grad_basis, grad_books)


def split_mesh(mesh):
    grid = np.asarray(mesh.devices)
    try:
        coords = np.array([d.coords for d in grid.reshape(-1)]).reshape(grid.shape + (-1,))
    except (AttributeError, ValueError):
        return None
    ny, nx, nz = (len(np.unique(coords[..., k])) for k in (1, 0, 2))
    if ny * nx * nz != grid.shape[0]:
        return None
    cube = coords.reshape(ny, nx, nz, grid.shape[1], -1)
    for axis, k in ((0, 1), (1, 0), (2, 2)):
        others = [c for c in range(3) if c != k]
        if np.any(np.diff(cube[..., others], axis=axis) != 0):
            return None
    return Mesh(grid.reshape(ny, nx, nz, grid.shape[1]), DOM + ("sub",)), (ny, nx, nz)


def solution(mesh):
    found = split_mesh(mesh)
    assert found is not None
    fine_mesh, (ny, nx, nz) = found
    dom_axes = ((("dy", "dx"), ny * nx), ("dz", nz))

    def run(*args):
        return shards(dom_axes, *args)

    rows = P(DOM + ("sub",))
    return jax.shard_map(
        run,
        mesh=fine_mesh,
        in_specs=(
            P(DOM + ("sub",), None),
            P("sub", None, None),
            P(),
            P(),
            P(),
            P(),
            P(DOM + ("sub",), None, None),
            rows,
            rows,
            P(DOM, "sub", None, None),
            P(DOM, "sub", None),
            P(),
            P(DOM + ("sub",), None),
        ),
        out_specs=(P(DOM + ("sub",), None), P(), P(), P(), P(), P("sub", None, None)),
        check_vma=False,
    )
```

```python
import jax
import jax.numpy as jnp
from jax import lax
from jax.sharding import Mesh, PartitionSpec as P
import numpy as np

TB = 128
TPB = 8
SLOT = 8
NHUB = 2
DOM = ("dy", "dx", "dz")


HIGHEST_PREC = lax.Precision.HIGHEST


def one_hot_codes(code_rows, code_count, out_type):
    return (code_rows[..., None] == jnp.arange(code_count, dtype=jnp.int32)).astype(out_type)


def decode(code_rows, complete_codebooks):
    indicator_rows = one_hot_codes(code_rows, complete_codebooks.shape[1], jnp.bfloat16)
    rows = jnp.einsum(
        "feu,euq->feq", indicator_rows, complete_codebooks, preferred_element_type=jnp.float32
    )
    return rows.astype(jnp.bfloat16).reshape(code_rows.shape[0], -1)


def fold_books(code_rows, gradients, code_count):
    book_count = code_rows.shape[1]
    slice_width = gradients.shape[1] // book_count
    codes_hot = jnp.arange(code_count, dtype=jnp.int32)
    folded = []
    for book_index in range(book_count):
        piece = gradients[:, book_index * slice_width : (book_index + 1) * slice_width]
        upper_bound = piece.astype(jnp.bfloat16)
        lower_bound = (piece - upper_bound.astype(jnp.float32)).astype(jnp.bfloat16)
        both = jnp.concatenate([upper_bound, lower_bound], axis=1)
        indicator_rows = (code_rows[:, book_index][:, None] == codes_hot).astype(jnp.bfloat16)
        summed = lax.dot_general(
            indicator_rows, both, (((0,), (0,)), ((), ())), preferred_element_type=jnp.float32
        )
        folded.append(summed[:, :slice_width] + summed[:, slice_width:])
    return jnp.stack(folded)


def all_sum(grad_w_msg, grad_w_self, part_alpha, part_basis, book_grad, dom_axes):
    sub_index = lax.axis_index("sub")
    width = grad_w_msg.shape[1]
    share = book_grad.shape[0] // 2
    dense = [grad_w_msg, grad_w_self, part_basis, part_alpha.reshape(-1, width)]

    def half_of(h):
        pieces = [lax.dynamic_slice_in_dim(x, h * (x.shape[0] // 2), x.shape[0] // 2, 0) for x in dense]
        pieces.append(lax.dynamic_slice_in_dim(book_grad, h * share, share, 0).reshape(-1, width))
        return jnp.concatenate(pieces, axis=0)

    swap = [(0, 1), (1, 0)]
    mine = half_of(sub_index) + lax.ppermute(half_of(1 - sub_index), "sub", swap)
    rows = mine.shape[0]
    shapes = []
    piece = mine
    for stage, (axis, size) in enumerate(dom_axes):
        shapes.append(piece.shape)
        lanes = piece.shape[-1]
        if piece.shape[0] % size:
            lanes = 256
        chunks = piece.reshape(size, -1, lanes)
        if stage == 0:
            chunks = chunks.astype(jnp.bfloat16)
        received = lax.all_to_all(chunks, axis, 0, 0, tiled=True)
        piece = jnp.sum(received.astype(jnp.float32), axis=0)
    piece = piece.astype(jnp.bfloat16)
    for (axis, size), shape in reversed(list(zip(dom_axes, shapes))):
        spread = jnp.broadcast_to(piece[None], (size,) + piece.shape)
        piece = lax.all_to_all(spread, axis, 0, 0, tiled=True).reshape(shape)
    own_half = piece
    dense_rows = rows - share * book_grad.shape[1] * book_grad.shape[2] // width
    own_dense = own_half[:dense_rows]
    other_dense = lax.ppermute(own_dense, "sub", swap)
    low = jnp.where(sub_index == 0, own_dense, other_dense).astype(jnp.float32)
    high = jnp.where(sub_index == 0, other_dense, own_dense).astype(jnp.float32)
    out = []
    start = 0
    for x in dense:
        r = x.shape[0] // 2
        out.append(jnp.concatenate([low[start : start + r], high[start : start + r]], axis=0))
        start += r
    out[3] = out[3].reshape(part_alpha.shape)
    books_mine = own_half[dense_rows:].astype(jnp.float32).reshape((share,) + book_grad.shape[1:])
    return out + [books_mine]


def shards(
    dom_axes,
    codes,
    books,
    alpha,
    basis,
    w_msg,
    w_self,
    tiles,
    tile_src,
    tile_rel,
    send_rows,
    send_count,
    hub_owner,
    cotangent,
):
    rows_dev, book_count = codes.shape
    code_count = books.shape[1]
    model_width = w_msg.shape[0]
    tile_count = tiles.shape[0]
    block_count = tile_count // TPB
    complete_codebooks = lax.all_gather(books, "sub", axis=0, tiled=True)
    rel_table = jnp.dot(alpha, basis, precision=HIGHEST_PREC, preferred_element_type=jnp.float32)
    targets = send_rows[0, 0]
    part_count = targets.shape[0]
    slot_valid = jnp.arange(SLOT, dtype=jnp.int32)[None, :] < send_count[0, 0][:, None]
    target_hot = one_hot_codes(targets.reshape(-1), rows_dev, jnp.bfloat16)
    picked_codes = jnp.dot(
        target_hot, codes.astype(jnp.bfloat16), preferred_element_type=jnp.float32
    ).astype(jnp.int32).reshape(targets.shape + (book_count,))
    out_codes = jnp.where(slot_valid[:, :, None], picked_codes, -1).reshape(part_count, -1)
    own_codes = jnp.broadcast_to(codes.reshape(1, -1), (part_count, codes.size))
    room = -(-(codes.size + out_codes.shape[1]) // 128) * 128
    filler = jnp.zeros((part_count, room - codes.size - out_codes.shape[1]), jnp.int32)
    payload = jnp.concatenate([own_codes, out_codes, filler], axis=1).astype(jnp.int16)
    incoming = lax.all_to_all(payload, DOM, 0, 0, tiled=True).astype(jnp.int32)
    recv_codes = incoming[:, codes.size : codes.size + out_codes.shape[1]].reshape(-1, book_count)
    hub_codes = [
        incoming[hub_owner[hub_index], : codes.size].reshape(codes.shape)
        for hub_index in range(NHUB)
    ]
    table_codes = jnp.concatenate([codes, recv_codes] + hub_codes, axis=0)
    local_rows = decode(codes, complete_codebooks)
    table = jnp.concatenate(
        [local_rows, decode(table_codes[rows_dev:], complete_codebooks)], axis=0
    )
    blocks = table.reshape(-1, TB, model_width)
    tile_blocks = tiles.reshape(block_count, TPB, TB, TB)
    picked = blocks[tile_src]
    scale = rel_table[tile_rel]
    composed = (picked.astype(jnp.float32) * scale[:, None, :]).astype(jnp.bfloat16)
    aggregate = jnp.einsum(
        "btij,btjd->bid",
        tile_blocks,
        composed.reshape(block_count, TPB, TB, model_width),
        preferred_element_type=jnp.float32,
    ).astype(jnp.bfloat16).reshape(rows_dev, model_width)
    pre_act = jnp.dot(aggregate, w_msg, preferred_element_type=jnp.float32) + jnp.dot(
        local_rows, w_self, preferred_element_type=jnp.float32
    )
    activated = jnp.tanh(pre_act)
    output = activated.astype(jnp.bfloat16)
    grad_pre = (cotangent.astype(jnp.float32) * (1.0 - activated * activated)).astype(jnp.bfloat16)
    contract_rows = (((0,), (0,)), ((), ()))
    contract_cols = (((1,), (1,)), ((), ()))
    grad_w_msg = lax.dot_general(
        aggregate, grad_pre, contract_rows, preferred_element_type=jnp.float32
    )
    grad_w_self = lax.dot_general(
        local_rows, grad_pre, contract_rows, preferred_element_type=jnp.float32
    )
    grad_agg = lax.dot_general(
        grad_pre, w_msg, contract_cols, preferred_element_type=jnp.float32
    ).astype(jnp.bfloat16)
    grad_self = lax.dot_general(grad_pre, w_self, contract_cols, preferred_element_type=jnp.float32)
    grad_blocks = grad_agg.reshape(block_count, TB, model_width)
    grad_comp = jnp.einsum(
        "btji,bjd->btid", tile_blocks, grad_blocks, preferred_element_type=jnp.float32
    ).reshape(tile_count, TB, model_width)
    rel_rows = jnp.sum(grad_comp * picked.astype(jnp.float32), axis=1)
    rel_grad = jnp.zeros(rel_table.shape, jnp.float32).at[tile_rel].add(rel_rows)
    tile_codes = table_codes.reshape(-1, TB, book_count)[tile_src].reshape(-1, book_count)
    contrib = (grad_comp * scale[:, None, :]).reshape(-1, model_width)
    book_grad = fold_books(tile_codes, contrib, code_count) + fold_books(codes, grad_self, code_count)
    part_alpha = jnp.dot(
        rel_grad, basis.T, precision=HIGHEST_PREC, preferred_element_type=jnp.float32
    )
    part_basis = jnp.dot(
        alpha.T, rel_grad, precision=HIGHEST_PREC, preferred_element_type=jnp.float32
    )
    total_msg, total_self, grad_basis, grad_alpha, grad_books = all_sum(
        grad_w_msg, grad_w_self, part_alpha, part_basis, book_grad, dom_axes
    )
    return (output, total_msg, total_self, grad_alpha, grad_basis, grad_books)


def split_mesh(mesh):
    grid = np.asarray(mesh.devices)
    try:
        coords = np.array([d.coords for d in grid.reshape(-1)]).reshape(grid.shape + (-1,))
    except (AttributeError, ValueError):
        return None
    ny, nx, nz = (len(np.unique(coords[..., k])) for k in (1, 0, 2))
    if ny * nx * nz != grid.shape[0]:
        return None
    cube = coords.reshape(ny, nx, nz, grid.shape[1], -1)
    for axis, k in ((0, 1), (1, 0), (2, 2)):
        others = [c for c in range(3) if c != k]
        if np.any(np.diff(cube[..., others], axis=axis) != 0):
            return None
    return Mesh(grid.reshape(ny, nx, nz, grid.shape[1]), DOM + ("sub",)), (ny, nx, nz)


def solution(mesh):
    found = split_mesh(mesh)
    assert found is not None
    fine_mesh, (ny, nx, nz) = found
    dom_axes = ((("dy", "dx"), ny * nx), ("dz", nz))

    def run(*args):
        return shards(dom_axes, *args)

    rows = P(DOM + ("sub",))
    return jax.shard_map(
        run,
        mesh=fine_mesh,
        in_specs=(
            P(DOM + ("sub",), None),
            P("sub", None, None),
            P(),
            P(),
            P(),
            P(),
            P(DOM + ("sub",), None, None),
            rows,
            rows,
            P(DOM, "sub", None, None),
            P(DOM, "sub", None),
            P(),
            P(DOM + ("sub",), None),
        ),
        out_specs=(P(DOM + ("sub",), None), P(), P(), P(), P(), P("sub", None, None)),
        check_vma=False,
    )
```

```python
import jax
import jax.numpy as jnp
from jax import lax
from jax.sharding import Mesh, PartitionSpec as P
import numpy as np

TB = 128
TPB = 8
SLOT = 8
NHUB = 2
DOM = ("dy", "dx", "dz")


HIGHEST_PREC = lax.Precision.HIGHEST


def one_hot_codes(code_rows, code_count, out_type):
    return (code_rows[..., None] == jnp.arange(code_count, dtype=jnp.int32)).astype(out_type)


def decode(code_rows, complete_codebooks):
    indicator_rows = one_hot_codes(code_rows, complete_codebooks.shape[1], jnp.bfloat16)
    rows = jnp.einsum(
        "feu,euq->feq", indicator_rows, complete_codebooks, preferred_element_type=jnp.float32
    )
    return rows.astype(jnp.bfloat16).reshape(code_rows.shape[0], -1)


def fold_books(code_rows, gradients, code_count):
    book_count = code_rows.shape[1]
    slice_width = gradients.shape[1] // book_count
    codes_hot = jnp.arange(code_count, dtype=jnp.int32)
    folded = []
    for book_index in range(book_count):
        piece = gradients[:, book_index * slice_width : (book_index + 1) * slice_width]
        upper_bound = piece.astype(jnp.bfloat16)
        lower_bound = (piece - upper_bound.astype(jnp.float32)).astype(jnp.bfloat16)
        both = jnp.concatenate([upper_bound, lower_bound], axis=1)
        indicator_rows = (code_rows[:, book_index][:, None] == codes_hot).astype(jnp.bfloat16)
        summed = lax.dot_general(
            indicator_rows, both, (((0,), (0,)), ((), ())), preferred_element_type=jnp.float32
        )
        folded.append(summed[:, :slice_width] + summed[:, slice_width:])
    return jnp.stack(folded)


def all_sum(grad_w_msg, grad_w_self, part_alpha, part_basis, book_grad, dom_axes):
    sub_index = lax.axis_index("sub")
    width = grad_w_msg.shape[1]
    share = book_grad.shape[0] // 2
    dense = [grad_w_msg, grad_w_self, part_basis, part_alpha.reshape(-1, width)]

    def half_of(h):
        pieces = [lax.dynamic_slice_in_dim(x, h * (x.shape[0] // 2), x.shape[0] // 2, 0) for x in dense]
        pieces.append(lax.dynamic_slice_in_dim(book_grad, h * share, share, 0).reshape(-1, width))
        return jnp.concatenate(pieces, axis=0)

    swap = [(0, 1), (1, 0)]
    sent = lax.ppermute(half_of(1 - sub_index).astype(jnp.bfloat16), "sub", swap)
    mine = half_of(sub_index) + sent.astype(jnp.float32)
    rows = mine.shape[0]
    shapes = []
    piece = mine
    for stage, (axis, size) in enumerate(dom_axes):
        shapes.append(piece.shape)
        lanes = piece.shape[-1]
        if piece.shape[0] % size:
            lanes = 256
        chunks = piece.reshape(size, -1, lanes)
        if stage == 0:
            chunks = chunks.astype(jnp.bfloat16)
        received = lax.all_to_all(chunks, axis, 0, 0, tiled=True)
        piece = jnp.sum(received.astype(jnp.float32), axis=0)
    piece = piece.astype(jnp.bfloat16)
    for (axis, size), shape in reversed(list(zip(dom_axes, shapes))):
        spread = jnp.broadcast_to(piece[None], (size,) + piece.shape)
        piece = lax.all_to_all(spread, axis, 0, 0, tiled=True).reshape(shape)
    own_half = piece
    dense_rows = rows - share * book_grad.shape[1] * book_grad.shape[2] // width
    own_dense = own_half[:dense_rows]
    other_dense = lax.ppermute(own_dense, "sub", swap)
    low = jnp.where(sub_index == 0, own_dense, other_dense).astype(jnp.float32)
    high = jnp.where(sub_index == 0, other_dense, own_dense).astype(jnp.float32)
    out = []
    start = 0
    for x in dense:
        r = x.shape[0] // 2
        out.append(jnp.concatenate([low[start : start + r], high[start : start + r]], axis=0))
        start += r
    out[3] = out[3].reshape(part_alpha.shape)
    books_mine = own_half[dense_rows:].astype(jnp.float32).reshape((share,) + book_grad.shape[1:])
    return out + [books_mine]


def shards(
    dom_axes,
    codes,
    books,
    alpha,
    basis,
    w_msg,
    w_self,
    tiles,
    tile_src,
    tile_rel,
    send_rows,
    send_count,
    hub_owner,
    cotangent,
):
    rows_dev, book_count = codes.shape
    code_count = books.shape[1]
    model_width = w_msg.shape[0]
    tile_count = tiles.shape[0]
    block_count = tile_count // TPB
    complete_codebooks = lax.all_gather(books, "sub", axis=0, tiled=True)
    rel_table = jnp.dot(alpha, basis, precision=HIGHEST_PREC, preferred_element_type=jnp.float32)
    targets = send_rows[0, 0]
    part_count = targets.shape[0]
    slot_valid = jnp.arange(SLOT, dtype=jnp.int32)[None, :] < send_count[0, 0][:, None]
    target_hot = one_hot_codes(targets.reshape(-1), rows_dev, jnp.bfloat16)
    picked_codes = jnp.dot(
        target_hot, codes.astype(jnp.bfloat16), preferred_element_type=jnp.float32
    ).astype(jnp.int32).reshape(targets.shape + (book_count,))
    out_codes = jnp.where(slot_valid[:, :, None], picked_codes, -1).reshape(part_count, -1)
    own_codes = jnp.broadcast_to(codes.reshape(1, -1), (part_count, codes.size))
    room = -(-(codes.size + out_codes.shape[1]) // 128) * 128
    filler = jnp.zeros((part_count, room - codes.size - out_codes.shape[1]), jnp.int32)
    payload = jnp.concatenate([own_codes, out_codes, filler], axis=1)
    incoming = lax.all_to_all(payload, DOM, 0, 0, tiled=True)
    recv_codes = incoming[:, codes.size : codes.size + out_codes.shape[1]].reshape(-1, book_count)
    hub_codes = [
        incoming[hub_owner[hub_index], : codes.size].reshape(codes.shape)
        for hub_index in range(NHUB)
    ]
    table_codes = jnp.concatenate([codes, recv_codes] + hub_codes, axis=0)
    local_rows = decode(codes, complete_codebooks)
    table = jnp.concatenate(
        [local_rows, decode(table_codes[rows_dev:], complete_codebooks)], axis=0
    )
    blocks = table.reshape(-1, TB, model_width)
    tile_blocks = tiles.reshape(block_count, TPB, TB, TB)
    picked = blocks[tile_src]
    scale = rel_table[tile_rel]
    composed = (picked.astype(jnp.float32) * scale[:, None, :]).astype(jnp.bfloat16)
    aggregate = jnp.einsum(
        "btij,btjd->bid",
        tile_blocks,
        composed.reshape(block_count, TPB, TB, model_width),
        preferred_element_type=jnp.float32,
    ).astype(jnp.bfloat16).reshape(rows_dev, model_width)
    pre_act = jnp.dot(aggregate, w_msg, preferred_element_type=jnp.float32) + jnp.dot(
        local_rows, w_self, preferred_element_type=jnp.float32
    )
    activated = jnp.tanh(pre_act)
    output = activated.astype(jnp.bfloat16)
    grad_pre = (cotangent.astype(jnp.float32) * (1.0 - activated * activated)).astype(jnp.bfloat16)
    contract_rows = (((0,), (0,)), ((), ()))
    contract_cols = (((1,), (1,)), ((), ()))
    grad_w_msg = lax.dot_general(
        aggregate, grad_pre, contract_rows, preferred_element_type=jnp.float32
    )
    grad_w_self = lax.dot_general(
        local_rows, grad_pre, contract_rows, preferred_element_type=jnp.float32
    )
    grad_agg = lax.dot_general(
        grad_pre, w_msg, contract_cols, preferred_element_type=jnp.float32
    ).astype(jnp.bfloat16)
    grad_self = lax.dot_general(grad_pre, w_self, contract_cols, preferred_element_type=jnp.float32)
    grad_blocks = grad_agg.reshape(block_count, TB, model_width)
    grad_comp = jnp.einsum(
        "btji,bjd->btid", tile_blocks, grad_blocks, preferred_element_type=jnp.float32
    ).reshape(tile_count, TB, model_width)
    rel_rows = jnp.sum(grad_comp * picked.astype(jnp.float32), axis=1)
    rel_grad = jnp.zeros(rel_table.shape, jnp.float32).at[tile_rel].add(rel_rows)
    tile_codes = table_codes.reshape(-1, TB, book_count)[tile_src].reshape(-1, book_count)
    contrib = (grad_comp * scale[:, None, :]).reshape(-1, model_width)
    book_grad = fold_books(tile_codes, contrib, code_count) + fold_books(codes, grad_self, code_count)
    part_alpha = jnp.dot(
        rel_grad, basis.T, precision=HIGHEST_PREC, preferred_element_type=jnp.float32
    )
    part_basis = jnp.dot(
        alpha.T, rel_grad, precision=HIGHEST_PREC, preferred_element_type=jnp.float32
    )
    total_msg, total_self, grad_basis, grad_alpha, grad_books = all_sum(
        grad_w_msg, grad_w_self, part_alpha, part_basis, book_grad, dom_axes
    )
    return (output, total_msg, total_self, grad_alpha, grad_basis, grad_books)


def split_mesh(mesh):
    grid = np.asarray(mesh.devices)
    try:
        coords = np.array([d.coords for d in grid.reshape(-1)]).reshape(grid.shape + (-1,))
    except (AttributeError, ValueError):
        return None
    ny, nx, nz = (len(np.unique(coords[..., k])) for k in (1, 0, 2))
    if ny * nx * nz != grid.shape[0]:
        return None
    cube = coords.reshape(ny, nx, nz, grid.shape[1], -1)
    for axis, k in ((0, 1), (1, 0), (2, 2)):
        others = [c for c in range(3) if c != k]
        if np.any(np.diff(cube[..., others], axis=axis) != 0):
            return None
    return Mesh(grid.reshape(ny, nx, nz, grid.shape[1]), DOM + ("sub",)), (ny, nx, nz)


def solution(mesh):
    found = split_mesh(mesh)
    assert found is not None
    fine_mesh, (ny, nx, nz) = found
    dom_axes = ((("dy", "dx"), ny * nx), ("dz", nz))

    def run(*args):
        return shards(dom_axes, *args)

    rows = P(DOM + ("sub",))
    return jax.shard_map(
        run,
        mesh=fine_mesh,
        in_specs=(
            P(DOM + ("sub",), None),
            P("sub", None, None),
            P(),
            P(),
            P(),
            P(),
            P(DOM + ("sub",), None, None),
            rows,
            rows,
            P(DOM, "sub", None, None),
            P(DOM, "sub", None),
            P(),
            P(DOM + ("sub",), None),
        ),
        out_specs=(P(DOM + ("sub",), None), P(), P(), P(), P(), P("sub", None, None)),
        check_vma=False,
    )
```

```python
import jax
import jax.numpy as jnp
from jax import lax
from jax.sharding import Mesh, PartitionSpec as P
import numpy as np

TB = 128
TPB = 8
SLOT = 8
NHUB = 2
DOM = ("dy", "dx", "dz")


HIGHEST_PREC = lax.Precision.HIGHEST


def one_hot_codes(code_rows, code_count, out_type):
    return (code_rows[..., None] == jnp.arange(code_count, dtype=jnp.int32)).astype(out_type)


def decode(code_rows, complete_codebooks):
    indicator_rows = one_hot_codes(code_rows, complete_codebooks.shape[1], jnp.bfloat16)
    rows = jnp.einsum(
        "feu,euq->feq", indicator_rows, complete_codebooks, preferred_element_type=jnp.float32
    )
    return rows.astype(jnp.bfloat16).reshape(code_rows.shape[0], -1)


def fold_books(code_rows, gradients, code_count):
    book_count = code_rows.shape[1]
    slice_width = gradients.shape[1] // book_count
    codes_hot = jnp.arange(code_count, dtype=jnp.int32)
    folded = []
    for book_index in range(book_count):
        piece = gradients[:, book_index * slice_width : (book_index + 1) * slice_width]
        upper_bound = piece.astype(jnp.bfloat16)
        lower_bound = (piece - upper_bound.astype(jnp.float32)).astype(jnp.bfloat16)
        both = jnp.concatenate([upper_bound, lower_bound], axis=1)
        indicator_rows = (code_rows[:, book_index][:, None] == codes_hot).astype(jnp.bfloat16)
        summed = lax.dot_general(
            indicator_rows, both, (((0,), (0,)), ((), ())), preferred_element_type=jnp.float32
        )
        folded.append(summed[:, :slice_width] + summed[:, slice_width:])
    return jnp.stack(folded)


def all_sum(grad_w_msg, grad_w_self, part_alpha, part_basis, book_grad, dom_axes):
    sub_index = lax.axis_index("sub")
    width = grad_w_msg.shape[1]
    share = book_grad.shape[0] // 2
    dense = [grad_w_msg, grad_w_self, part_basis, part_alpha.reshape(-1, width)]

    def half_of(h):
        pieces = [lax.dynamic_slice_in_dim(x, h * (x.shape[0] // 2), x.shape[0] // 2, 0) for x in dense]
        pieces.append(lax.dynamic_slice_in_dim(book_grad, h * share, share, 0).reshape(-1, width))
        return jnp.concatenate(pieces, axis=0)

    swap = [(0, 1), (1, 0)]
    mine = half_of(sub_index) + lax.ppermute(half_of(1 - sub_index), "sub", swap)
    rows = mine.shape[0]
    shapes = []
    piece = mine
    for stage, (axis, size) in enumerate(dom_axes):
        shapes.append(piece.shape)
        lanes = piece.shape[-1]
        if piece.shape[0] % size:
            lanes = 256
        chunks = piece.reshape(size, -1, lanes)
        if stage == 0:
            chunks = chunks.astype(jnp.bfloat16)
        received = lax.all_to_all(chunks, axis, 0, 0, tiled=True)
        piece = jnp.sum(received.astype(jnp.float32), axis=0)
    piece = piece.astype(jnp.bfloat16)
    for (axis, size), shape in reversed(list(zip(dom_axes, shapes))):
        spread = jnp.broadcast_to(piece[None], (size,) + piece.shape)
        piece = lax.all_to_all(spread, axis, 0, 0, tiled=True).reshape(shape)
    own_half = piece
    dense_rows = rows - share * book_grad.shape[1] * book_grad.shape[2] // width
    own_dense = own_half[:dense_rows]
    other_dense = lax.ppermute(own_dense, "sub", swap)
    low = jnp.where(sub_index == 0, own_dense, other_dense).astype(jnp.float32)
    high = jnp.where(sub_index == 0, other_dense, own_dense).astype(jnp.float32)
    out = []
    start = 0
    for x in dense:
        r = x.shape[0] // 2
        out.append(jnp.concatenate([low[start : start + r], high[start : start + r]], axis=0))
        start += r
    out[3] = out[3].reshape(part_alpha.shape)
    books_mine = own_half[dense_rows:].astype(jnp.float32).reshape((share,) + book_grad.shape[1:])
    return out + [books_mine]


def shards(
    dom_axes,
    codes,
    books,
    alpha,
    basis,
    w_msg,
    w_self,
    tiles,
    tile_src,
    tile_rel,
    send_rows,
    send_count,
    hub_owner,
    cotangent,
):
    rows_dev, book_count = codes.shape
    code_count = books.shape[1]
    model_width = w_msg.shape[0]
    tile_count = tiles.shape[0]
    block_count = tile_count // TPB
    complete_codebooks = lax.all_gather(books, "sub", axis=0, tiled=True)
    rel_table = jnp.dot(alpha, basis, precision=HIGHEST_PREC, preferred_element_type=jnp.float32)
    targets = send_rows[0, 0]
    part_count = targets.shape[0]
    slot_valid = jnp.arange(SLOT, dtype=jnp.int32)[None, :] < send_count[0, 0][:, None]
    target_hot = one_hot_codes(targets.reshape(-1), rows_dev, jnp.bfloat16)
    picked_codes = jnp.dot(
        target_hot, codes.astype(jnp.bfloat16), preferred_element_type=jnp.float32
    ).astype(jnp.int32).reshape(targets.shape + (book_count,))
    out_codes = jnp.where(slot_valid[:, :, None], picked_codes, -1).reshape(part_count, -1)
    own_codes = jnp.broadcast_to(codes.reshape(1, -1), (part_count, codes.size))
    room = -(-(codes.size + out_codes.shape[1]) // 128) * 128
    filler = jnp.zeros((part_count, room - codes.size - out_codes.shape[1]), jnp.int32)
    payload = jnp.concatenate([own_codes, out_codes, filler], axis=1)
    incoming = lax.all_to_all(payload, DOM, 0, 0, tiled=True)
    local_rows = decode(codes, complete_codebooks)
    self_part = jnp.dot(local_rows, w_self, preferred_element_type=jnp.float32)
    scale = rel_table[tile_rel]
    incoming, self_part, scale = lax.optimization_barrier((incoming, self_part, scale))
    recv_codes = incoming[:, codes.size : codes.size + out_codes.shape[1]].reshape(-1, book_count)
    hub_codes = [
        incoming[hub_owner[hub_index], : codes.size].reshape(codes.shape)
        for hub_index in range(NHUB)
    ]
    table_codes = jnp.concatenate([codes, recv_codes] + hub_codes, axis=0)
    table = jnp.concatenate(
        [local_rows, decode(table_codes[rows_dev:], complete_codebooks)], axis=0
    )
    blocks = table.reshape(-1, TB, model_width)
    tile_blocks = tiles.reshape(block_count, TPB, TB, TB)
    picked = blocks[tile_src]
    composed = (picked.astype(jnp.float32) * scale[:, None, :]).astype(jnp.bfloat16)
    aggregate = jnp.einsum(
        "btij,btjd->bid",
        tile_blocks,
        composed.reshape(block_count, TPB, TB, model_width),
        preferred_element_type=jnp.float32,
    ).astype(jnp.bfloat16).reshape(rows_dev, model_width)
    pre_act = jnp.dot(aggregate, w_msg, preferred_element_type=jnp.float32) + self_part
    activated = jnp.tanh(pre_act)
    output = activated.astype(jnp.bfloat16)
    grad_pre = (cotangent.astype(jnp.float32) * (1.0 - activated * activated)).astype(jnp.bfloat16)
    contract_rows = (((0,), (0,)), ((), ()))
    contract_cols = (((1,), (1,)), ((), ()))
    grad_w_msg = lax.dot_general(
        aggregate, grad_pre, contract_rows, preferred_element_type=jnp.float32
    )
    grad_w_self = lax.dot_general(
        local_rows, grad_pre, contract_rows, preferred_element_type=jnp.float32
    )
    grad_agg = lax.dot_general(
        grad_pre, w_msg, contract_cols, preferred_element_type=jnp.float32
    ).astype(jnp.bfloat16)
    grad_self = lax.dot_general(grad_pre, w_self, contract_cols, preferred_element_type=jnp.float32)
    grad_blocks = grad_agg.reshape(block_count, TB, model_width)
    grad_comp = jnp.einsum(
        "btji,bjd->btid", tile_blocks, grad_blocks, preferred_element_type=jnp.float32
    ).reshape(tile_count, TB, model_width)
    rel_rows = jnp.sum(grad_comp * picked.astype(jnp.float32), axis=1)
    rel_grad = jnp.zeros(rel_table.shape, jnp.float32).at[tile_rel].add(rel_rows)
    tile_codes = table_codes.reshape(-1, TB, book_count)[tile_src].reshape(-1, book_count)
    contrib = (grad_comp * scale[:, None, :]).reshape(-1, model_width)
    book_grad = fold_books(tile_codes, contrib, code_count) + fold_books(codes, grad_self, code_count)
    part_alpha = jnp.dot(
        rel_grad, basis.T, precision=HIGHEST_PREC, preferred_element_type=jnp.float32
    )
    part_basis = jnp.dot(
        alpha.T, rel_grad, precision=HIGHEST_PREC, preferred_element_type=jnp.float32
    )
    total_msg, total_self, grad_basis, grad_alpha, grad_books = all_sum(
        grad_w_msg, grad_w_self, part_alpha, part_basis, book_grad, dom_axes
    )
    return (output, total_msg, total_self, grad_alpha, grad_basis, grad_books)


def split_mesh(mesh):
    grid = np.asarray(mesh.devices)
    try:
        coords = np.array([d.coords for d in grid.reshape(-1)]).reshape(grid.shape + (-1,))
    except (AttributeError, ValueError):
        return None
    ny, nx, nz = (len(np.unique(coords[..., k])) for k in (1, 0, 2))
    if ny * nx * nz != grid.shape[0]:
        return None
    cube = coords.reshape(ny, nx, nz, grid.shape[1], -1)
    for axis, k in ((0, 1), (1, 0), (2, 2)):
        others = [c for c in range(3) if c != k]
        if np.any(np.diff(cube[..., others], axis=axis) != 0):
            return None
    return Mesh(grid.reshape(ny, nx, nz, grid.shape[1]), DOM + ("sub",)), (ny, nx, nz)


def solution(mesh):
    found = split_mesh(mesh)
    assert found is not None
    fine_mesh, (ny, nx, nz) = found
    dom_axes = ((("dy", "dx"), ny * nx), ("dz", nz))

    def run(*args):
        return shards(dom_axes, *args)

    rows = P(DOM + ("sub",))
    return jax.shard_map(
        run,
        mesh=fine_mesh,
        in_specs=(
            P(DOM + ("sub",), None),
            P("sub", None, None),
            P(),
            P(),
            P(),
            P(),
            P(DOM + ("sub",), None, None),
            rows,
            rows,
            P(DOM, "sub", None, None),
            P(DOM, "sub", None),
            P(),
            P(DOM + ("sub",), None),
        ),
        out_specs=(P(DOM + ("sub",), None), P(), P(), P(), P(), P("sub", None, None)),
        check_vma=False,
    )
```

```python
import jax
import jax.numpy as jnp
from jax import lax
from jax.sharding import Mesh, PartitionSpec as P
import numpy as np

TB = 128
TPB = 8
SLOT = 8
NHUB = 2
DOM = ("dy", "dx", "dz")


HIGHEST_PREC = lax.Precision.HIGHEST


def one_hot_codes(code_rows, code_count, out_type):
    return (code_rows[..., None] == jnp.arange(code_count, dtype=jnp.int32)).astype(out_type)


def decode(code_rows, complete_codebooks):
    indicator_rows = one_hot_codes(code_rows, complete_codebooks.shape[1], jnp.bfloat16)
    rows = jnp.einsum(
        "feu,euq->feq", indicator_rows, complete_codebooks, preferred_element_type=jnp.float32
    )
    return rows.astype(jnp.bfloat16).reshape(code_rows.shape[0], -1)


def fold_books(code_rows, gradients, code_count):
    book_count = code_rows.shape[1]
    slice_width = gradients.shape[1] // book_count
    codes_hot = jnp.arange(code_count, dtype=jnp.int32)
    folded = []
    for book_index in range(book_count):
        piece = gradients[:, book_index * slice_width : (book_index + 1) * slice_width]
        upper_bound = piece.astype(jnp.bfloat16)
        lower_bound = (piece - upper_bound.astype(jnp.float32)).astype(jnp.bfloat16)
        both = jnp.concatenate([upper_bound, lower_bound], axis=1)
        indicator_rows = (code_rows[:, book_index][:, None] == codes_hot).astype(jnp.bfloat16)
        summed = lax.dot_general(
            indicator_rows, both, (((0,), (0,)), ((), ())), preferred_element_type=jnp.float32
        )
        folded.append(summed[:, :slice_width] + summed[:, slice_width:])
    return jnp.stack(folded)


def all_sum(grad_w_msg, grad_w_self, part_alpha, part_basis, book_grad, dom_axes):
    sub_index = lax.axis_index("sub")
    width = grad_w_msg.shape[1]
    share = book_grad.shape[0] // 2
    dense = [grad_w_msg, grad_w_self, part_basis, part_alpha.reshape(-1, width)]

    def half_of(h):
        pieces = [lax.dynamic_slice_in_dim(x, h * (x.shape[0] // 2), x.shape[0] // 2, 0) for x in dense]
        pieces.append(lax.dynamic_slice_in_dim(book_grad, h * share, share, 0).reshape(-1, width))
        return jnp.concatenate(pieces, axis=0)

    swap = [(0, 1), (1, 0)]
    mine = half_of(sub_index) + lax.ppermute(half_of(1 - sub_index), "sub", swap)
    rows = mine.shape[0]
    shapes = []
    piece = mine
    for axis, size in dom_axes:
        shapes.append(piece.shape)
        lanes = piece.shape[-1]
        if piece.shape[0] % size:
            lanes = 256
        chunks = piece.reshape(size, -1, lanes)
        chunks = chunks.astype(jnp.bfloat16)
        received = lax.all_to_all(chunks, axis, 0, 0, tiled=True)
        piece = jnp.sum(received.astype(jnp.float32), axis=0)
    piece = piece.astype(jnp.bfloat16)
    for (axis, size), shape in reversed(list(zip(dom_axes, shapes))):
        spread = jnp.broadcast_to(piece[None], (size,) + piece.shape)
        piece = lax.all_to_all(spread, axis, 0, 0, tiled=True).reshape(shape)
    own_half = piece
    dense_rows = rows - share * book_grad.shape[1] * book_grad.shape[2] // width
    own_dense = own_half[:dense_rows]
    other_dense = lax.ppermute(own_dense, "sub", swap)
    low = jnp.where(sub_index == 0, own_dense, other_dense).astype(jnp.float32)
    high = jnp.where(sub_index == 0, other_dense, own_dense).astype(jnp.float32)
    out = []
    start = 0
    for x in dense:
        r = x.shape[0] // 2
        out.append(jnp.concatenate([low[start : start + r], high[start : start + r]], axis=0))
        start += r
    out[3] = out[3].reshape(part_alpha.shape)
    books_mine = own_half[dense_rows:].astype(jnp.float32).reshape((share,) + book_grad.shape[1:])
    return out + [books_mine]


def shards(
    dom_axes,
    codes,
    books,
    alpha,
    basis,
    w_msg,
    w_self,
    tiles,
    tile_src,
    tile_rel,
    send_rows,
    send_count,
    hub_owner,
    cotangent,
):
    rows_dev, book_count = codes.shape
    code_count = books.shape[1]
    model_width = w_msg.shape[0]
    tile_count = tiles.shape[0]
    block_count = tile_count // TPB
    complete_codebooks = lax.all_gather(books, "sub", axis=0, tiled=True)
    rel_table = jnp.dot(alpha, basis, precision=HIGHEST_PREC, preferred_element_type=jnp.float32)
    targets = send_rows[0, 0]
    part_count = targets.shape[0]
    slot_valid = jnp.arange(SLOT, dtype=jnp.int32)[None, :] < send_count[0, 0][:, None]
    target_hot = one_hot_codes(targets.reshape(-1), rows_dev, jnp.bfloat16)
    picked_codes = jnp.dot(
        target_hot, codes.astype(jnp.bfloat16), preferred_element_type=jnp.float32
    ).astype(jnp.int32).reshape(targets.shape + (book_count,))
    out_codes = jnp.where(slot_valid[:, :, None], picked_codes, -1).reshape(part_count, -1)
    own_codes = jnp.broadcast_to(codes.reshape(1, -1), (part_count, codes.size))
    room = -(-(codes.size + out_codes.shape[1]) // 128) * 128
    filler = jnp.zeros((part_count, room - codes.size - out_codes.shape[1]), jnp.int32)
    payload = jnp.concatenate([own_codes, out_codes, filler], axis=1)
    incoming = lax.all_to_all(payload, DOM, 0, 0, tiled=True)
    local_rows = decode(codes, complete_codebooks)
    self_part = jnp.dot(local_rows, w_self, preferred_element_type=jnp.float32)
    scale = rel_table[tile_rel]
    incoming, self_part, scale = lax.optimization_barrier((incoming, self_part, scale))
    recv_codes = incoming[:, codes.size : codes.size + out_codes.shape[1]].reshape(-1, book_count)
    hub_codes = [
        incoming[hub_owner[hub_index], : codes.size].reshape(codes.shape)
        for hub_index in range(NHUB)
    ]
    table_codes = jnp.concatenate([codes, recv_codes] + hub_codes, axis=0)
    table = jnp.concatenate(
        [local_rows, decode(table_codes[rows_dev:], complete_codebooks)], axis=0
    )
    blocks = table.reshape(-1, TB, model_width)
    tile_blocks = tiles.reshape(block_count, TPB, TB, TB)
    picked = blocks[tile_src]
    composed = (picked.astype(jnp.float32) * scale[:, None, :]).astype(jnp.bfloat16)
    aggregate = jnp.einsum(
        "btij,btjd->bid",
        tile_blocks,
        composed.reshape(block_count, TPB, TB, model_width),
        preferred_element_type=jnp.float32,
    ).astype(jnp.bfloat16).reshape(rows_dev, model_width)
    pre_act = jnp.dot(aggregate, w_msg, preferred_element_type=jnp.float32) + self_part
    activated = jnp.tanh(pre_act)
    output = activated.astype(jnp.bfloat16)
    grad_pre = (cotangent.astype(jnp.float32) * (1.0 - activated * activated)).astype(jnp.bfloat16)
    contract_rows = (((0,), (0,)), ((), ()))
    contract_cols = (((1,), (1,)), ((), ()))
    grad_w_msg = lax.dot_general(
        aggregate, grad_pre, contract_rows, preferred_element_type=jnp.float32
    )
    grad_w_self = lax.dot_general(
        local_rows, grad_pre, contract_rows, preferred_element_type=jnp.float32
    )
    grad_agg = lax.dot_general(
        grad_pre, w_msg, contract_cols, preferred_element_type=jnp.float32
    ).astype(jnp.bfloat16)
    grad_self = lax.dot_general(grad_pre, w_self, contract_cols, preferred_element_type=jnp.float32)
    grad_blocks = grad_agg.reshape(block_count, TB, model_width)
    grad_comp = jnp.einsum(
        "btji,bjd->btid", tile_blocks, grad_blocks, preferred_element_type=jnp.float32
    ).reshape(tile_count, TB, model_width)
    rel_rows = jnp.sum(grad_comp * picked.astype(jnp.float32), axis=1)
    rel_grad = jnp.zeros(rel_table.shape, jnp.float32).at[tile_rel].add(rel_rows)
    tile_codes = table_codes.reshape(-1, TB, book_count)[tile_src].reshape(-1, book_count)
    contrib = (grad_comp * scale[:, None, :]).reshape(-1, model_width)
    book_grad = fold_books(tile_codes, contrib, code_count) + fold_books(codes, grad_self, code_count)
    part_alpha = jnp.dot(
        rel_grad, basis.T, precision=HIGHEST_PREC, preferred_element_type=jnp.float32
    )
    part_basis = jnp.dot(
        alpha.T, rel_grad, precision=HIGHEST_PREC, preferred_element_type=jnp.float32
    )
    total_msg, total_self, grad_basis, grad_alpha, grad_books = all_sum(
        grad_w_msg, grad_w_self, part_alpha, part_basis, book_grad, dom_axes
    )
    return (output, total_msg, total_self, grad_alpha, grad_basis, grad_books)


def split_mesh(mesh):
    grid = np.asarray(mesh.devices)
    try:
        coords = np.array([d.coords for d in grid.reshape(-1)]).reshape(grid.shape + (-1,))
    except (AttributeError, ValueError):
        return None
    ny, nx, nz = (len(np.unique(coords[..., k])) for k in (1, 0, 2))
    if ny * nx * nz != grid.shape[0]:
        return None
    cube = coords.reshape(ny, nx, nz, grid.shape[1], -1)
    for axis, k in ((0, 1), (1, 0), (2, 2)):
        others = [c for c in range(3) if c != k]
        if np.any(np.diff(cube[..., others], axis=axis) != 0):
            return None
    return Mesh(grid.reshape(ny, nx, nz, grid.shape[1]), DOM + ("sub",)), (ny, nx, nz)


def solution(mesh):
    found = split_mesh(mesh)
    assert found is not None
    fine_mesh, (ny, nx, nz) = found
    dom_axes = ((("dy", "dx"), ny * nx), ("dz", nz))

    def run(*args):
        return shards(dom_axes, *args)

    rows = P(DOM + ("sub",))
    return jax.shard_map(
        run,
        mesh=fine_mesh,
        in_specs=(
            P(DOM + ("sub",), None),
            P("sub", None, None),
            P(),
            P(),
            P(),
            P(),
            P(DOM + ("sub",), None, None),
            rows,
            rows,
            P(DOM, "sub", None, None),
            P(DOM, "sub", None),
            P(),
            P(DOM + ("sub",), None),
        ),
        out_specs=(P(DOM + ("sub",), None), P(), P(), P(), P(), P("sub", None, None)),
        check_vma=False,
    )
```
